32 devices in a mesh: seq: 16 (over z, y, core), dp: 2 (over x).
Axes of the slice: x: 2, y: 2, z: 4, core: 2. Of those that a mesh axis runs over, the one named last changes fastest.
Arguments:
- queries: bfloat16 [2, 3072, 1536], P('dp', 'seq'), may hold values from -100 to 100
- key_vectors: bfloat16 [2, 3072, 1536], P('dp', 'seq'), may hold values from -6 to 6
- value_vectors: bfloat16 [2, 3072, 1536], P('dp', 'seq'), may hold values from -48 to 48
- w_out: bfloat16 [1536, 1536], P(('seq', 'dp')), may hold values from -0.15625 to 0.15625
- cotangent: bfloat16 [2, 3072, 1536], P('dp', 'seq'), may hold values from -0.119628906 to 0.119628906
Outputs:
- projected: bfloat16 [2, 3072, 1536], P('dp', 'seq')
- grad_w_out: float32 [1536, 1536], P(('seq', 'dp'))
The draws below stay inside these ranges and needn't reach their ends.
All inputs are finite; a program needn't handle non-finite values.
Results may differ from the reference program's by a relative error of at most 0.0055.
Values may be sent and summed in bfloat16 or wider, within the bound.
No kernel may reach another device: no remote copies, remote signals or barrier semaphores. Data moves between devices by JAX's collectives and lax.ppermute only.
A program may use at most 128 MiB of HBM per device.

```python
import jax
import jax.numpy as jnp
from jax import lax

D = 1536
HEADS = 8
HEAD_DIM = 192
BINS = 3072
SEQS = 2


def pair_draw(key):
    first_key, second_key = jax.random.split(jax.random.fold_in(key, 7), 2)
    full_shape = (SEQS, BINS, D)
    base_q = jnp.clip(1.5 * jax.random.normal(first_key, full_shape, jnp.float32), -9.0, 9.0)
    base_k = jnp.clip(jax.random.normal(second_key, full_shape, jnp.float32), -6.0, 6.0)
    return (base_q, base_k)


def draw_queries(key, part):
    return pair_draw(key)[0].astype(jnp.bfloat16)


def draw_key_vectors(key, part):
    return pair_draw(key)[1].astype(jnp.bfloat16)


def steps_of(key, extent, pieces, least, high):
    level = 1.0
    for axis_at, shards_of in pieces:
        draws = jax.random.uniform(jax.random.fold_in(jax.random.fold_in(key, 6), axis_at), (shards_of,), jnp.float32, least / len(pieces), high / len(pieces))
        level = level * jnp.repeat(jnp.exp(draws), extent[axis_at] // shards_of).reshape((-1,) + (1,) * (len(extent) - 1 - axis_at))
    return level


def scatter_about(rng, extent, scale, bound, shards=(), dtype=jnp.bfloat16):
    factor_of = steps_of(rng, extent, shards, -0.22, 0.18) if shards else 1.0
    entries = jax.random.normal(rng, extent, jnp.float32) * scale * factor_of
    return jnp.minimum(jnp.maximum(entries, -bound), bound).astype(dtype)


def setup_inputs(seed: int = 0) -> dict:
    key_of = jax.random.split(jax.random.key(seed), 6)
    queries = draw_queries(jax.random.fold_in(key_of[5], 71), 0)
    key_vectors = draw_key_vectors(jax.random.fold_in(key_of[5], 71), 0)
    value_vectors = scatter_about(key_of[2], (SEQS, BINS, D), 8.0, 48.0, ((0, 2), (1, 16)))
    w_out = scatter_about(key_of[3], (D, D), D ** -0.5, 0.15625, ((0, 32),))
    cotangent = scatter_about(key_of[4], (SEQS, BINS, D), 0.02, 0.119628906, ((0, 2), (1, 16)))
    return dict(queries=queries, key_vectors=key_vectors, value_vectors=value_vectors, w_out=w_out, cotangent=cotangent)


def attend_head(query_head, key_head, value_head):
    score_scale = HEAD_DIM ** -0.5
    block_size = min(512, BINS)

    def one_block(query_block):
        scores = jnp.dot(query_block, key_head.T, preferred_element_type=jnp.float32) * score_scale
        largest = jnp.max(scores, axis=1, keepdims=True)
        raised = jnp.exp(scores - largest)
        denominator = jnp.sum(raised, axis=1, keepdims=True)
        weights = raised.astype(jnp.bfloat16)
        mixed = jnp.dot(weights, value_head, preferred_element_type=jnp.float32)
        return (mixed / denominator).astype(jnp.bfloat16)

    blocks = lax.map(one_block, query_head.reshape(BINS // block_size, block_size, HEAD_DIM))
    return blocks.reshape(BINS, HEAD_DIM)


def by_head(tensor):
    return tensor.reshape(SEQS, BINS, HEADS, HEAD_DIM).transpose(0, 2, 1, 3).reshape(SEQS * HEADS, BINS, HEAD_DIM)


def reference(queries, key_vectors, value_vectors, w_out, cotangent):
    stacked = (by_head(queries), by_head(key_vectors), by_head(value_vectors))
    attended = lax.map(lambda triple: attend_head(triple[0], triple[1], triple[2]), stacked)
    attended = attended.reshape(SEQS, HEADS, BINS, HEAD_DIM).transpose(0, 2, 1, 3).reshape(SEQS * BINS, D)
    projected = jnp.dot(attended, w_out, preferred_element_type=jnp.float32).astype(jnp.bfloat16)
    projected = projected.reshape(SEQS, BINS, D)
    grad_w_out = lax.dot_general(attended, cotangent.reshape(SEQS * BINS, D), (((0,), (0,)), ((), ())), preferred_element_type=jnp.float32)
    return projected, grad_w_out
```

```python
import jax
import jax.numpy as jnp
from jax import lax
from jax.sharding import PartitionSpec as P

HEADS = 8
HEAD_DIM = 192


def attend(query_here, key_all, value_all):
    query_count = query_here.shape[0]
    head_width = query_here.shape[1]
    block_size = min(512, query_count)
    score_scale = HEAD_DIM ** (-0.5)

    def one_block(query_block):
        scores = jnp.dot(query_block, key_all.T, preferred_element_type=jnp.float32) * score_scale
        largest = jnp.max(scores, axis=1, keepdims=True)
        raised = jnp.exp(scores - largest)
        denominator = jnp.sum(raised, axis=1, keepdims=True)
        weights = raised.astype(jnp.bfloat16)
        mixed = jnp.dot(weights, value_all, preferred_element_type=jnp.float32)
        return (mixed / denominator).astype(jnp.bfloat16)

    blocks = lax.map(
        one_block, query_here.reshape(query_count // block_size, block_size, head_width)
    )
    return blocks.reshape(query_count, head_width)


def local(queries, key_vectors, value_vectors, w_out, cotangent):
    head_count = HEADS
    head_width = HEAD_DIM
    seq_count = lax.axis_size("seq")
    dp_count = lax.axis_size("dp")
    per_head = seq_count // head_count
    row_count = queries.shape[1]
    sub = row_count // per_head
    width = queries.shape[2]

    w_full = lax.all_gather(w_out, ("seq", "dp"), axis=0, tiled=True)

    def a2a(tensor):
        return lax.all_to_all(tensor, "seq", split_axis=0, concat_axis=0, tiled=True)

    query_slots = (
        queries[0]
        .reshape(per_head, sub, head_count, head_width)
        .transpose(2, 0, 1, 3)
        .reshape(seq_count, sub, head_width)
    )

    def head_slots(tensor):
        tensor = tensor[0].reshape(row_count, head_count, head_width).transpose(1, 0, 2)
        tensor = jnp.broadcast_to(
            tensor[:, None], (head_count, per_head, row_count, head_width)
        )
        return tensor.reshape(seq_count, row_count, head_width)

    cot_slots = jnp.broadcast_to(
        cotangent[0].reshape(1, per_head, sub, width), (head_count, per_head, sub, width)
    ).reshape(seq_count, sub, width)

    got_query = a2a(query_slots)
    got_key = a2a(head_slots(key_vectors))
    got_value = a2a(head_slots(value_vectors))
    got_cot = a2a(cot_slots)

    query_here = got_query.reshape(seq_count * sub, head_width)
    key_all = got_key.reshape(seq_count * row_count, head_width)
    value_all = got_value.reshape(seq_count * row_count, head_width)
    cot_here = got_cot.reshape(seq_count * sub, width)

    attended_here = attend(query_here, key_all, value_all)

    partial = lax.dot_general(
        attended_here, cot_here, (((0,), (0,)), ((), ())), preferred_element_type=jnp.float32
    )

    returned = a2a(attended_here.reshape(seq_count, sub, head_width))
    attended = (
        returned.reshape(head_count, per_head, sub, head_width)
        .transpose(1, 2, 0, 3)
        .reshape(row_count, width)
    )
    projected = jnp.dot(attended, w_full, preferred_element_type=jnp.float32).astype(
        jnp.bfloat16
    )

    seq_index = lax.axis_index("seq")
    group = seq_index % per_head
    chunk = head_width // per_head
    pieces = partial.reshape(per_head, chunk, width)
    summed = lax.dynamic_index_in_dim(pieces, group, axis=0, keepdims=False)
    if per_head > 1:
        for step in range(1, per_head):
            target = (group + step) % per_head
            outgoing = lax.dynamic_index_in_dim(pieces, target, axis=0, keepdims=False)
            perm = [
                (s, (s // per_head) * per_head + (s % per_head + step) % per_head)
                for s in range(seq_count)
            ]
            summed = summed + lax.ppermute(outgoing, "seq", perm)
    grad_w_out = lax.psum_scatter(summed, "dp", scatter_dimension=0, tiled=True)
    return (projected.reshape(1, row_count, width), grad_w_out)


def solution(mesh):
    placed = (
        P("dp", "seq", None),
        P("dp", "seq", None),
        P("dp", "seq", None),
        P(("seq", "dp"), None),
        P("dp", "seq", None),
    )
    return jax.shard_map(
        local,
        mesh=mesh,
        in_specs=placed,
        out_specs=(P("dp", "seq", None), P(("seq", "dp"), None)),
        check_vma=False,
    )
```

```python
import jax
import jax.numpy as jnp
from jax import lax
from jax.sharding import Mesh
from jax.sharding import PartitionSpec as P

HEADS = 8
HEAD_DIM = 192


def attend(query_here, key_all, value_all):
    query_count = query_here.shape[0]
    head_width = query_here.shape[1]
    block_size = min(512, query_count)
    score_scale = HEAD_DIM ** (-0.5)

    def one_block(query_block):
        scores = jnp.dot(query_block, key_all.T, preferred_element_type=jnp.float32) * score_scale
        largest = jnp.max(scores, axis=1, keepdims=True)
        raised = jnp.exp(scores - largest)
        denominator = jnp.sum(raised, axis=1, keepdims=True)
        weights = raised.astype(jnp.bfloat16)
        mixed = jnp.dot(weights, value_all, preferred_element_type=jnp.float32)
        return (mixed / denominator).astype(jnp.bfloat16)

    blocks = lax.map(
        one_block, query_here.reshape(query_count // block_size, block_size, head_width)
    )
    return blocks.reshape(query_count, head_width)


ALL = ("side", "inner", "dp")


def local(queries, key_vectors, value_vectors, w_out, cotangent):
    head_count = HEADS
    head_width = HEAD_DIM
    side_count = lax.axis_size("side")
    dp_count = lax.axis_size("dp")
    row_count = queries.shape[1]
    width = queries.shape[2]

    w_full = lax.all_gather(w_out, ALL, axis=0, tiled=True)
    cot_side = lax.all_gather(cotangent[0], "inner", axis=0, tiled=True)

    def a2a(tensor):
        return lax.all_to_all(tensor, "inner", split_axis=0, concat_axis=0, tiled=True)

    def by_head(tensor):
        return tensor[0].reshape(row_count, head_count, head_width).transpose(1, 0, 2)

    query_here = a2a(by_head(queries)).reshape(head_count * row_count, head_width)
    key_side = a2a(by_head(key_vectors)).reshape(head_count * row_count, head_width)
    value_side = a2a(by_head(value_vectors)).reshape(head_count * row_count, head_width)
    key_all = lax.all_gather(key_side, "side", axis=0, tiled=True)
    value_all = lax.all_gather(value_side, "side", axis=0, tiled=True)

    attended_here = attend(query_here, key_all, value_all)

    partial = lax.dot_general(
        attended_here, cot_side, (((0,), (0,)), ((), ())), preferred_element_type=jnp.float32
    )

    returned = a2a(attended_here.reshape(head_count, row_count, head_width))
    attended = returned.transpose(1, 0, 2).reshape(row_count, width)
    projected = jnp.dot(attended, w_full, preferred_element_type=jnp.float32).astype(
        jnp.bfloat16
    )

    seq_count = side_count * head_count
    if side_count == dp_count:
        reduced = lax.psum_scatter(partial, "dp", scatter_dimension=0, tiled=True)
        reduced = lax.psum_scatter(reduced, "side", scatter_dimension=0, tiled=True)
        perm = []
        for g in range(side_count):
            for h in range(head_count):
                for p in range(dp_count):
                    source = (g * head_count + h) * dp_count + p
                    target = (side_count * h + p) * dp_count + g
                    perm.append((source, target))
        grad_w_out = lax.ppermute(reduced, ALL, perm)
    else:
        reduced = lax.psum_scatter(partial, "side", scatter_dimension=0, tiled=True)
        reduced = lax.psum_scatter(reduced, "dp", scatter_dimension=0, tiled=True)
        perm = [
            (g * head_count + h, side_count * h + g)
            for g in range(side_count)
            for h in range(head_count)
        ]
        grad_w_out = lax.ppermute(reduced, ("side", "inner"), perm)
    del seq_count
    return (projected.reshape(1, row_count, width), grad_w_out)


def solution(mesh):
    seq_count = mesh.shape["seq"]
    dp_count = mesh.shape["dp"]
    fine = Mesh(
        mesh.devices.reshape(seq_count // HEADS, HEADS, dp_count), ("side", "inner", "dp")
    )
    seq = ("side", "inner")
    placed = (
        P("dp", seq, None),
        P("dp", seq, None),
        P("dp", seq, None),
        P(ALL, None),
        P("dp", seq, None),
    )
    return jax.shard_map(
        local,
        mesh=fine,
        in_specs=placed,
        out_specs=(P("dp", seq, None), P(ALL, None)),
        check_vma=False,
    )
```

```python
import jax
import jax.numpy as jnp
from jax import lax
from jax.sharding import Mesh
from jax.sharding import PartitionSpec as P

HEADS = 8
HEAD_DIM = 192


def attend(query_here, key_all, value_all):
    query_count = query_here.shape[0]
    head_width = query_here.shape[1]
    block_size = min(512, query_count)
    score_scale = HEAD_DIM ** (-0.5)

    def one_block(query_block):
        scores = jnp.dot(query_block, key_all.T, preferred_element_type=jnp.float32) * score_scale
        largest = jnp.max(scores, axis=1, keepdims=True)
        raised = jnp.exp(scores - largest)
        denominator = jnp.sum(raised, axis=1, keepdims=True)
        weights = raised.astype(jnp.bfloat16)
        mixed = jnp.dot(weights, value_all, preferred_element_type=jnp.float32)
        return (mixed / denominator).astype(jnp.bfloat16)

    blocks = lax.map(
        one_block, query_here.reshape(query_count // block_size, block_size, head_width)
    )
    return blocks.reshape(query_count, head_width)


ALL = ("side", "inner", "dp")


def local(queries, key_vectors, value_vectors, w_out, cotangent):
    head_count = HEADS
    head_width = HEAD_DIM
    side_count = lax.axis_size("side")
    dp_count = lax.axis_size("dp")
    row_count = queries.shape[1]
    width = queries.shape[2]

    w_full = lax.all_gather(w_out, ALL, axis=0, tiled=True)
    cot_side = lax.all_gather(cotangent[0], "inner", axis=0, tiled=True)

    def a2a(tensor):
        return lax.all_to_all(tensor, "inner", split_axis=0, concat_axis=0, tiled=True)

    def by_head(tensor):
        return tensor[0].reshape(row_count, head_count, head_width).transpose(1, 0, 2)

    side_index = lax.axis_index("side")
    stacked = jnp.concatenate(
        [by_head(queries), by_head(key_vectors), by_head(value_vectors)], axis=2
    )
    got = a2a(stacked).reshape(head_count * row_count, 3 * head_width)
    query_here = got[:, :head_width]
    kv_side = got[:, head_width:]
    kv_parts = [kv_side]
    for step in range(1, side_count):
        perm = [(g, (g + step) % side_count) for g in range(side_count)]
        kv_parts.append(lax.ppermute(kv_side, "side", perm))
    kv_all = jnp.concatenate(kv_parts, axis=0)
    key_all = kv_all[:, :head_width]
    value_all = kv_all[:, head_width:]
    del side_index

    attended_here = attend(query_here, key_all, value_all)

    partial = lax.dot_general(
        attended_here, cot_side, (((0,), (0,)), ((), ())), preferred_element_type=jnp.float32
    )

    returned = a2a(attended_here.reshape(head_count, row_count, head_width))
    attended = returned.transpose(1, 0, 2).reshape(row_count, width)
    projected = jnp.dot(attended, w_full, preferred_element_type=jnp.float32).astype(
        jnp.bfloat16
    )

    chunk_count = side_count * dp_count
    chunk = head_width // chunk_count
    pieces = partial.reshape(chunk_count, chunk, width)
    side_index = lax.axis_index("side")
    dp_index = lax.axis_index("dp")
    holder = side_index * dp_count + dp_index
    grad_w_out = None
    for step in range(chunk_count):
        perm = []
        for g in range(side_count):
            for h in range(head_count):
                for p in range(dp_count):
                    c = (g * dp_count + p + step) % chunk_count
                    source = (g * head_count + h) * dp_count + p
                    target = (side_count * h + c // dp_count) * dp_count + c % dp_count
                    perm.append((source, target))
        outgoing = lax.dynamic_index_in_dim(
            pieces, (holder + step) % chunk_count, axis=0, keepdims=False
        )
        arrived = lax.ppermute(outgoing, ALL, perm)
        grad_w_out = arrived if grad_w_out is None else grad_w_out + arrived
    return (projected.reshape(1, row_count, width), grad_w_out)


def solution(mesh):
    seq_count = mesh.shape["seq"]
    dp_count = mesh.shape["dp"]
    fine = Mesh(
        mesh.devices.reshape(seq_count // HEADS, HEADS, dp_count), ("side", "inner", "dp")
    )
    seq = ("side", "inner")
    placed = (
        P("dp", seq, None),
        P("dp", seq, None),
        P("dp", seq, None),
        P(ALL, None),
        P("dp", seq, None),
    )
    return jax.shard_map(
        local,
        mesh=fine,
        in_specs=placed,
        out_specs=(P("dp", seq, None), P(ALL, None)),
        check_vma=False,
    )
```

```python
import jax
import jax.numpy as jnp
from jax import lax
from jax.sharding import Mesh
from jax.sharding import PartitionSpec as P

HEADS = 8
HEAD_DIM = 192


def attend(query_here, key_all, value_all):
    query_count = query_here.shape[0]
    head_width = query_here.shape[1]
    block_size = min(512, query_count)
    score_scale = HEAD_DIM ** (-0.5)

    def one_block(query_block):
        scores = jnp.dot(query_block, key_all.T, preferred_element_type=jnp.float32) * score_scale
        largest = jnp.max(scores, axis=1, keepdims=True)
        raised = jnp.exp(scores - largest)
        denominator = jnp.sum(raised, axis=1, keepdims=True)
        weights = raised.astype(jnp.bfloat16)
        mixed = jnp.dot(weights, value_all, preferred_element_type=jnp.float32)
        return (mixed / denominator).astype(jnp.bfloat16)

    blocks = lax.map(
        one_block, query_here.reshape(query_count // block_size, block_size, head_width)
    )
    return blocks.reshape(query_count, head_width)


ALL = ("side", "chip", "core", "dp")
INNER = ("chip", "core")


def local(queries, key_vectors, value_vectors, w_out, cotangent):
    head_count = HEADS
    head_width = HEAD_DIM
    side_count = lax.axis_size("side")
    dp_count = lax.axis_size("dp")
    row_count = queries.shape[1]
    width = queries.shape[2]

    chip_count = lax.axis_size("chip")
    core_count = lax.axis_size("core")

    def with_partner(tensor):
        core_index = lax.axis_index("core")
        other = lax.ppermute(tensor, "core", [(0, 1), (1, 0)])
        first = jnp.where(core_index == 0, tensor, other)
        second = jnp.where(core_index == 0, other, tensor)
        return jnp.stack([first, second])

    w_core = lax.all_gather(w_out, ("side", "chip", "dp"), axis=0, tiled=True)
    w_full = (
        with_partner(w_core)
        .reshape(core_count, side_count, chip_count, dp_count, w_out.shape[0], width)
        .transpose(1, 2, 0, 3, 4, 5)
        .reshape(w_out.shape[0] * side_count * chip_count * core_count * dp_count, width)
    )
    cot_core = lax.all_gather(cotangent[0], "chip", axis=0, tiled=True)
    cot_side = with_partner(cot_core).reshape(core_count * chip_count * row_count, width)

    def a2a(tensor):
        return lax.all_to_all(tensor, INNER, split_axis=0, concat_axis=0, tiled=True)

    def by_head(tensor):
        return tensor[0].reshape(row_count, head_count, head_width).transpose(1, 0, 2)

    stacked = jnp.concatenate(
        [by_head(queries), by_head(key_vectors), by_head(value_vectors)], axis=2
    )
    got = a2a(stacked).reshape(head_count * row_count, 3 * head_width)
    query_here = got[:, :head_width]
    kv_side = got[:, head_width:]
    kv_parts = [kv_side]
    for step in range(1, side_count):
        perm = [(g, (g + step) % side_count) for g in range(side_count)]
        kv_parts.append(lax.ppermute(kv_side, "side", perm))
    kv_all = jnp.concatenate(kv_parts, axis=0)
    key_all = kv_all[:, :head_width]
    value_all = kv_all[:, head_width:]

    attended_here = attend(query_here, key_all, value_all)

    attended_rows = (
        attended_here.reshape(chip_count, core_count, row_count, head_width)
        .transpose(1, 0, 2, 3)
        .reshape(core_count * chip_count * row_count, head_width)
    )
    partial = lax.dot_general(
        attended_rows, cot_side, (((0,), (0,)), ((), ())), preferred_element_type=jnp.float32
    )

    returned = a2a(attended_here.reshape(head_count, row_count, head_width))
    attended = returned.transpose(1, 0, 2).reshape(row_count, width)
    projected = jnp.dot(attended, w_full, preferred_element_type=jnp.float32).astype(
        jnp.bfloat16
    )

    chunk_count = side_count * dp_count
    chunk = head_width // chunk_count
    pieces = partial.reshape(chunk_count, chunk, width)
    side_index = lax.axis_index("side")
    dp_index = lax.axis_index("dp")
    holder = side_index * dp_count + dp_index
    grad_w_out = None
    for step in range(chunk_count):
        perm = []
        for g in range(side_count):
            for h in range(head_count):
                for p in range(dp_count):
                    c = (g * dp_count + p + step) % chunk_count
                    source = (g * head_count + h) * dp_count + p
                    target = (side_count * h + c // dp_count) * dp_count + c % dp_count
                    perm.append((source, target))
        outgoing = lax.dynamic_index_in_dim(
            pieces, (holder + step) % chunk_count, axis=0, keepdims=False
        )
        arrived = lax.ppermute(outgoing, ALL, perm)
        grad_w_out = arrived if grad_w_out is None else grad_w_out + arrived
    return (projected.reshape(1, row_count, width), grad_w_out)


def solution(mesh):
    seq_count = mesh.shape["seq"]
    dp_count = mesh.shape["dp"]
    fine = Mesh(
        mesh.devices.reshape(seq_count // HEADS, HEADS // 2, 2, dp_count), ALL
    )
    seq = ("side", "chip", "core")
    placed = (
        P("dp", seq, None),
        P("dp", seq, None),
        P("dp", seq, None),
        P(ALL, None),
        P("dp", seq, None),
    )
    return jax.shard_map(
        local,
        mesh=fine,
        in_specs=placed,
        out_specs=(P("dp", seq, None), P(ALL, None)),
        check_vma=False,
    )
```

```python
import jax
import jax.numpy as jnp
from jax import lax
from jax.sharding import Mesh
from jax.sharding import PartitionSpec as P

HEADS = 8
HEAD_DIM = 192


def attend(query_here, key_all, value_all):
    query_count = query_here.shape[0]
    head_width = query_here.shape[1]
    block_size = min(512, query_count)
    score_scale = HEAD_DIM ** (-0.5)

    def one_block(query_block):
        scores = jnp.dot(query_block, key_all.T, preferred_element_type=jnp.float32) * score_scale
        largest = jnp.max(scores, axis=1, keepdims=True)
        raised = jnp.exp(scores - largest)
        denominator = jnp.sum(raised, axis=1, keepdims=True)
        weights = raised.astype(jnp.bfloat16)
        mixed = jnp.dot(weights, value_all, preferred_element_type=jnp.float32)
        return (mixed / denominator).astype(jnp.bfloat16)

    blocks = lax.map(
        one_block, query_here.reshape(query_count // block_size, block_size, head_width)
    )
    return blocks.reshape(query_count, head_width)


ALL = ("side", "chip", "core", "dp")
INNER = ("chip", "core")


def local(queries, key_vectors, value_vectors, w_out, cotangent):
    head_count = HEADS
    head_width = HEAD_DIM
    side_count = lax.axis_size("side")
    dp_count = lax.axis_size("dp")
    row_count = queries.shape[1]
    width = queries.shape[2]

    chip_count = lax.axis_size("chip")
    core_count = lax.axis_size("core")

    def with_partner(tensor):
        core_index = lax.axis_index("core")
        other = lax.ppermute(tensor, "core", [(0, 1), (1, 0)])
        first = jnp.where(core_index == 0, tensor, other)
        second = jnp.where(core_index == 0, other, tensor)
        return jnp.stack([first, second])

    w_core = lax.all_gather(w_out, ("side", "chip", "dp"), axis=0, tiled=True)
    cot_core = lax.all_gather(cotangent[0], "chip", axis=0, tiled=True)
    cot_side = with_partner(cot_core).reshape(core_count * chip_count * row_count, width)

    def a2a(tensor):
        return lax.all_to_all(tensor, INNER, split_axis=0, concat_axis=0, tiled=True)

    def by_head(tensor):
        return tensor[0].reshape(row_count, head_count, head_width).transpose(1, 0, 2)

    kv_raw = jnp.concatenate([by_head(key_vectors), by_head(value_vectors)], axis=2)
    kv_crossed = [
        lax.ppermute(kv_raw, "side", [(g, (g + step) % side_count) for g in range(side_count)])
        for step in range(1, side_count)
    ]
    stacked = jnp.concatenate([by_head(queries), kv_raw], axis=2)
    got = a2a(stacked).reshape(head_count * row_count, 3 * head_width)
    query_here = got[:, :head_width]
    kv_parts = [got[:, head_width:]]
    for crossed in kv_crossed:
        kv_parts.append(a2a(crossed).reshape(head_count * row_count, 2 * head_width))
    kv_all = jnp.concatenate(kv_parts, axis=0)
    key_all = kv_all[:, :head_width]
    value_all = kv_all[:, head_width:]

    attended_here = attend(query_here, key_all, value_all)

    attended_rows = (
        attended_here.reshape(chip_count, core_count, row_count, head_width)
        .transpose(1, 0, 2, 3)
        .reshape(core_count * chip_count * row_count, head_width)
    )
    partial = lax.dot_general(
        attended_rows, cot_side, (((0,), (0,)), ((), ())), preferred_element_type=jnp.float32
    )

    returned = a2a(attended_here.reshape(head_count, row_count, head_width))
    attended = returned.transpose(1, 0, 2).reshape(row_count, width)
    core_index = lax.axis_index("core")
    by_core = attended.reshape(
        row_count, side_count, chip_count, core_count, dp_count, w_out.shape[0]
    )
    mine = lax.dynamic_index_in_dim(by_core, core_index, axis=3, keepdims=False)
    theirs = lax.dynamic_index_in_dim(by_core, 1 - core_index, axis=3, keepdims=False)
    w_partner = lax.ppermute(w_core, "core", [(0, 1), (1, 0)])
    projected = (
        jnp.dot(mine.reshape(row_count, -1), w_core, preferred_element_type=jnp.float32)
        + jnp.dot(theirs.reshape(row_count, -1), w_partner, preferred_element_type=jnp.float32)
    ).astype(jnp.bfloat16)

    chunk_count = side_count * dp_count
    chunk = head_width // chunk_count
    pieces = partial.reshape(chunk_count, chunk, width)
    side_index = lax.axis_index("side")
    dp_index = lax.axis_index("dp")
    holder = side_index * dp_count + dp_index
    grad_w_out = None
    for step in range(chunk_count):
        perm = []
        for g in range(side_count):
            for h in range(head_count):
                for p in range(dp_count):
                    c = (g * dp_count + p + step) % chunk_count
                    source = (g * head_count + h) * dp_count + p
                    target = (side_count * h + c // dp_count) * dp_count + c % dp_count
                    perm.append((source, target))
        outgoing = lax.dynamic_index_in_dim(
            pieces, (holder + step) % chunk_count, axis=0, keepdims=False
        )
        arrived = lax.ppermute(outgoing, ALL, perm)
        grad_w_out = arrived if grad_w_out is None else grad_w_out + arrived
    return (projected.reshape(1, row_count, width), grad_w_out)


def solution(mesh):
    seq_count = mesh.shape["seq"]
    dp_count = mesh.shape["dp"]
    fine = Mesh(
        mesh.devices.reshape(seq_count // HEADS, HEADS // 2, 2, dp_count), ALL
    )
    seq = ("side", "chip", "core")
    placed = (
        P("dp", seq, None),
        P("dp", seq, None),
        P("dp", seq, None),
        P(ALL, None),
        P("dp", seq, None),
    )
    return jax.shard_map(
        local,
        mesh=fine,
        in_specs=placed,
        out_specs=(P("dp", seq, None), P(ALL, None)),
        check_vma=False,
    )
```

```python
import jax
import jax.numpy as jnp
from jax import lax
from jax.sharding import Mesh
from jax.sharding import PartitionSpec as P

HEADS = 8
HEAD_DIM = 192


def attend(query_here, key_all, value_all):
    query_count = query_here.shape[0]
    head_width = query_here.shape[1]
    block_size = min(512, query_count)
    score_scale = HEAD_DIM ** (-0.5)

    def one_block(query_block):
        scores = jnp.dot(query_block, key_all.T, preferred_element_type=jnp.float32) * score_scale
        largest = jnp.max(scores, axis=1, keepdims=True)
        raised = jnp.exp(scores - largest)
        denominator = jnp.sum(raised, axis=1, keepdims=True)
        weights = raised.astype(jnp.bfloat16)
        mixed = jnp.dot(weights, value_all, preferred_element_type=jnp.float32)
        return (mixed / denominator).astype(jnp.bfloat16)

    blocks = lax.map(
        one_block, query_here.reshape(query_count // block_size, block_size, head_width)
    )
    return blocks.reshape(query_count, head_width)


ALL = ("side", "inner", "dp")


def local(queries, key_vectors, value_vectors, w_out, cotangent):
    head_count = HEADS
    head_width = HEAD_DIM
    side_count = lax.axis_size("side")
    dp_count = lax.axis_size("dp")
    row_count = queries.shape[1]
    width = queries.shape[2]

    dp_index = lax.axis_index("dp")
    w_other = lax.ppermute(w_out, "dp", [(p, (p + 1) % dp_count) for p in range(dp_count)])
    if dp_count == 2:
        w_pair = jnp.stack(
            [jnp.where(dp_index == 0, w_out, w_other), jnp.where(dp_index == 0, w_other, w_out)]
        )
        w_full = lax.all_gather(w_pair, ("side", "inner"), axis=0, tiled=True).reshape(-1, width)
    else:
        w_full = lax.all_gather(w_out, ALL, axis=0, tiled=True)
    cot_side = lax.all_gather(cotangent[0], "inner", axis=0, tiled=True)

    def a2a(tensor):
        return lax.all_to_all(tensor, "inner", split_axis=0, concat_axis=0, tiled=True)

    def by_head(tensor):
        return tensor[0].reshape(row_count, head_count, head_width).transpose(1, 0, 2)

    side_index = lax.axis_index("side")
    stacked = jnp.concatenate(
        [by_head(queries), by_head(key_vectors), by_head(value_vectors)], axis=2
    )
    got = a2a(stacked).reshape(head_count * row_count, 3 * head_width)
    query_here = got[:, :head_width]
    kv_side = got[:, head_width:]
    kv_parts = [kv_side]
    for step in range(1, side_count):
        perm = [(g, (g + step) % side_count) for g in range(side_count)]
        kv_parts.append(lax.ppermute(kv_side, "side", perm))
    kv_all = jnp.concatenate(kv_parts, axis=0)
    key_all = kv_all[:, :head_width]
    value_all = kv_all[:, head_width:]
    del side_index

    attended_here = attend(query_here, key_all, value_all)

    partial = lax.dot_general(
        attended_here, cot_side, (((0,), (0,)), ((), ())), preferred_element_type=jnp.float32
    )

    returned = a2a(attended_here.reshape(head_count, row_count, head_width))
    attended = returned.transpose(1, 0, 2).reshape(row_count, width)
    projected = jnp.dot(attended, w_full, preferred_element_type=jnp.float32).astype(
        jnp.bfloat16
    )

    chunk_count = side_count * dp_count
    chunk = head_width // chunk_count
    side_index = lax.axis_index("side")
    if dp_count == 2:
        pieces = partial.reshape(side_count, dp_count, chunk, width)
        kept = lax.dynamic_index_in_dim(pieces, dp_index, axis=1, keepdims=False)
        sent = lax.dynamic_index_in_dim(pieces, 1 - dp_index, axis=1, keepdims=False)
        kept = kept + lax.ppermute(sent, "dp", [(0, 1), (1, 0)])
        grad_w_out = None
        for step in range(side_count):
            perm = []
            for g in range(side_count):
                for h in range(head_count):
                    for p in range(dp_count):
                        owner_side = (g + step) % side_count
                        source = (g * head_count + h) * dp_count + p
                        target = (side_count * h + owner_side) * dp_count + p
                        perm.append((source, target))
            outgoing = lax.dynamic_index_in_dim(
                kept, (side_index + step) % side_count, axis=0, keepdims=False
            )
            arrived = lax.ppermute(outgoing, ALL, perm)
            grad_w_out = arrived if grad_w_out is None else grad_w_out + arrived
    else:
        pieces = partial.reshape(chunk_count, chunk, width)
        holder = side_index * dp_count + dp_index
        grad_w_out = None
        for step in range(chunk_count):
            perm = []
            for g in range(side_count):
                for h in range(head_count):
                    for p in range(dp_count):
                        c = (g * dp_count + p + step) % chunk_count
                        source = (g * head_count + h) * dp_count + p
                        target = (side_count * h + c // dp_count) * dp_count + c % dp_count
                        perm.append((source, target))
            outgoing = lax.dynamic_index_in_dim(
                pieces, (holder + step) % chunk_count, axis=0, keepdims=False
            )
            arrived = lax.ppermute(outgoing, ALL, perm)
            grad_w_out = arrived if grad_w_out is None else grad_w_out + arrived
    return (projected.reshape(1, row_count, width), grad_w_out)


def solution(mesh):
    seq_count = mesh.shape["seq"]
    dp_count = mesh.shape["dp"]
    fine = Mesh(
        mesh.devices.reshape(seq_count // HEADS, HEADS, dp_count), ("side", "inner", "dp")
    )
    seq = ("side", "inner")
    placed = (
        P("dp", seq, None),
        P("dp", seq, None),
        P("dp", seq, None),
        P(ALL, None),
        P("dp", seq, None),
    )
    return jax.shard_map(
        local,
        mesh=fine,
        in_specs=placed,
        out_specs=(P("dp", seq, None), P(ALL, None)),
        check_vma=False,
    )
```

```python
import jax
import jax.numpy as jnp
from jax import lax
from jax.sharding import Mesh
from jax.sharding import PartitionSpec as P

HEADS = 8
HEAD_DIM = 192


def attend(query_here, key_all, value_all):
    query_count = query_here.shape[0]
    head_width = query_here.shape[1]
    block_size = min(512, query_count)
    score_scale = HEAD_DIM ** (-0.5)

    def one_block(query_block):
        scores = jnp.dot(query_block, key_all.T, preferred_element_type=jnp.float32) * score_scale
        largest = jnp.max(scores, axis=1, keepdims=True)
        raised = jnp.exp(scores - largest)
        denominator = jnp.sum(raised, axis=1, keepdims=True)
        weights = raised.astype(jnp.bfloat16)
        mixed = jnp.dot(weights, value_all, preferred_element_type=jnp.float32)
        return (mixed / denominator).astype(jnp.bfloat16)

    blocks = lax.map(
        one_block, query_here.reshape(query_count // block_size, block_size, head_width)
    )
    return blocks.reshape(query_count, head_width)


ALL = ("side", "chip", "core", "dp")
INNER = ("chip", "core")


def local(queries, key_vectors, value_vectors, w_out, cotangent):
    head_count = HEADS
    head_width = HEAD_DIM
    side_count = lax.axis_size("side")
    dp_count = lax.axis_size("dp")
    row_count = queries.shape[1]
    width = queries.shape[2]

    dp_index = lax.axis_index("dp")
    w_other = lax.ppermute(w_out, "dp", [(p, (p + 1) % dp_count) for p in range(dp_count)])
    if dp_count == 2:
        w_pair = jnp.stack(
            [jnp.where(dp_index == 0, w_out, w_other), jnp.where(dp_index == 0, w_other, w_out)]
        )
        w_full = lax.all_gather(w_pair, ("side", "chip", "core"), axis=0, tiled=True).reshape(-1, width)
    else:
        w_full = lax.all_gather(w_out, ALL, axis=0, tiled=True)
    chip_count = lax.axis_size("chip")
    core_count = lax.axis_size("core")
    core_index = lax.axis_index("core")
    cot_core = lax.all_gather(cotangent[0], "chip", axis=0, tiled=True)
    cot_other = lax.ppermute(cot_core, "core", [(0, 1), (1, 0)])
    cot_side = jnp.concatenate(
        [
            jnp.where(core_index == 0, cot_core, cot_other),
            jnp.where(core_index == 0, cot_other, cot_core),
        ],
        axis=0,
    )

    def a2a(tensor):
        return lax.all_to_all(tensor, INNER, split_axis=0, concat_axis=0, tiled=True)

    def by_head(tensor):
        return tensor[0].reshape(row_count, head_count, head_width).transpose(1, 0, 2)

    side_index = lax.axis_index("side")
    stacked = jnp.concatenate(
        [by_head(queries), by_head(key_vectors), by_head(value_vectors)], axis=2
    )
    got = a2a(stacked).reshape(head_count * row_count, 3 * head_width)
    query_here = got[:, :head_width]
    kv_side = got[:, head_width:]
    kv_parts = [kv_side]
    for step in range(1, side_count):
        perm = [(g, (g + step) % side_count) for g in range(side_count)]
        kv_parts.append(lax.ppermute(kv_side, "side", perm))
    kv_all = jnp.concatenate(kv_parts, axis=0)
    key_all = kv_all[:, :head_width]
    value_all = kv_all[:, head_width:]
    del side_index

    attended_here = attend(query_here, key_all, value_all)

    attended_rows = (
        attended_here.reshape(chip_count, core_count, row_count, head_width)
        .transpose(1, 0, 2, 3)
        .reshape(core_count * chip_count * row_count, head_width)
    )
    partial = lax.dot_general(
        attended_rows, cot_side, (((0,), (0,)), ((), ())), preferred_element_type=jnp.float32
    )

    returned = a2a(attended_here.reshape(head_count, row_count, head_width))
    attended = returned.transpose(1, 0, 2).reshape(row_count, width)
    projected = jnp.dot(attended, w_full, preferred_element_type=jnp.float32).astype(
        jnp.bfloat16
    )

    chunk_count = side_count * dp_count
    chunk = head_width // chunk_count
    side_index = lax.axis_index("side")
    if dp_count == 2:
        pieces = partial.reshape(side_count, dp_count, chunk, width)
        kept = lax.dynamic_index_in_dim(pieces, dp_index, axis=1, keepdims=False)
        sent = lax.dynamic_index_in_dim(pieces, 1 - dp_index, axis=1, keepdims=False)
        kept = kept + lax.ppermute(sent, "dp", [(0, 1), (1, 0)])
        grad_w_out = None
        for step in range(side_count):
            perm = []
            for g in range(side_count):
                for h in range(head_count):
                    for p in range(dp_count):
                        owner_side = (g + step) % side_count
                        source = (g * head_count + h) * dp_count + p
                        target = (side_count * h + owner_side) * dp_count + p
                        perm.append((source, target))
            outgoing = lax.dynamic_index_in_dim(
                kept, (side_index + step) % side_count, axis=0, keepdims=False
            )
            arrived = lax.ppermute(outgoing, ALL, perm)
            grad_w_out = arrived if grad_w_out is None else grad_w_out + arrived
    else:
        pieces = partial.reshape(chunk_count, chunk, width)
        holder = side_index * dp_count + dp_index
        grad_w_out = None
        for step in range(chunk_count):
            perm = []
            for g in range(side_count):
                for h in range(head_count):
                    for p in range(dp_count):
                        c = (g * dp_count + p + step) % chunk_count
                        source = (g * head_count + h) * dp_count + p
                        target = (side_count * h + c // dp_count) * dp_count + c % dp_count
                        perm.append((source, target))
            outgoing = lax.dynamic_index_in_dim(
                pieces, (holder + step) % chunk_count, axis=0, keepdims=False
            )
            arrived = lax.ppermute(outgoing, ALL, perm)
            grad_w_out = arrived if grad_w_out is None else grad_w_out + arrived
    return (projected.reshape(1, row_count, width), grad_w_out)


def solution(mesh):
    seq_count = mesh.shape["seq"]
    dp_count = mesh.shape["dp"]
    fine = Mesh(mesh.devices.reshape(seq_count // HEADS, HEADS // 2, 2, dp_count), ALL)
    seq = ("side", "chip", "core")
    placed = (
        P("dp", seq, None),
        P("dp", seq, None),
        P("dp", seq, None),
        P(ALL, None),
        P("dp", seq, None),
    )
    return jax.shard_map(
        local,
        mesh=fine,
        in_specs=placed,
        out_specs=(P("dp", seq, None), P(ALL, None)),
        check_vma=False,
    )
```

```python
import jax
import jax.numpy as jnp
from jax import lax
from jax.sharding import Mesh
from jax.sharding import PartitionSpec as P

HEADS = 8
HEAD_DIM = 192


def attend(query_here, key_all, value_all):
    query_count = query_here.shape[0]
    head_width = query_here.shape[1]
    block_size = min(512, query_count)
    score_scale = HEAD_DIM ** (-0.5)

    def one_block(query_block):
        scores = jnp.dot(query_block, key_all.T, preferred_element_type=jnp.float32) * score_scale
        largest = jnp.max(scores, axis=1, keepdims=True)
        raised = jnp.exp(scores - largest)
        denominator = jnp.sum(raised, axis=1, keepdims=True)
        weights = raised.astype(jnp.bfloat16)
        mixed = jnp.dot(weights, value_all, preferred_element_type=jnp.float32)
        return (mixed / denominator).astype(jnp.bfloat16)

    blocks = lax.map(
        one_block, query_here.reshape(query_count // block_size, block_size, head_width)
    )
    return blocks.reshape(query_count, head_width)


ALL = ("side", "inner", "dp")


def local(queries, key_vectors, value_vectors, w_out, cotangent):
    head_count = HEADS
    head_width = HEAD_DIM
    side_count = lax.axis_size("side")
    dp_count = lax.axis_size("dp")
    row_count = queries.shape[1]
    width = queries.shape[2]

    dp_index = lax.axis_index("dp")
    w_other = lax.ppermute(w_out, "dp", [(p, (p + 1) % dp_count) for p in range(dp_count)])
    if dp_count == 2:
        w_pair = jnp.stack(
            [jnp.where(dp_index == 0, w_out, w_other), jnp.where(dp_index == 0, w_other, w_out)]
        )
        w_full = lax.all_gather(w_pair, ("side", "inner"), axis=0, tiled=True).reshape(-1, width)
    else:
        w_full = lax.all_gather(w_out, ALL, axis=0, tiled=True)
    cot_side = lax.all_gather(cotangent[0], "inner", axis=0, tiled=True)

    def a2a(tensor):
        return lax.all_to_all(tensor, "inner", split_axis=0, concat_axis=0, tiled=True)

    def by_head(tensor):
        return tensor[0].reshape(row_count, head_count, head_width).transpose(1, 0, 2)

    side_index = lax.axis_index("side")
    kv_raw = jnp.concatenate([by_head(key_vectors), by_head(value_vectors)], axis=2)
    kv_crossed = [
        lax.ppermute(kv_raw, "side", [(g, (g + step) % side_count) for g in range(side_count)])
        for step in range(1, side_count)
    ]
    stacked = jnp.concatenate([by_head(queries), kv_raw], axis=2)
    got = a2a(stacked).reshape(head_count * row_count, 3 * head_width)
    query_here = got[:, :head_width]
    kv_parts = [got[:, head_width:]]
    for crossed in kv_crossed:
        kv_parts.append(a2a(crossed).reshape(head_count * row_count, 2 * head_width))
    kv_all = jnp.concatenate(kv_parts, axis=0)
    key_all = kv_all[:, :head_width]
    value_all = kv_all[:, head_width:]

    attended_here = attend(query_here, key_all, value_all)

    partial = lax.dot_general(
        attended_here, cot_side, (((0,), (0,)), ((), ())), preferred_element_type=jnp.float32
    )

    returned = a2a(attended_here.reshape(head_count, row_count, head_width))
    attended = returned.transpose(1, 0, 2).reshape(row_count, width)
    projected = jnp.dot(attended, w_full, preferred_element_type=jnp.float32).astype(
        jnp.bfloat16
    )

    chunk_count = side_count * dp_count
    chunk = head_width // chunk_count
    side_index = lax.axis_index("side")
    if dp_count == 2:
        pieces = partial.reshape(side_count, dp_count, chunk, width)
        kept = lax.dynamic_index_in_dim(pieces, dp_index, axis=1, keepdims=False)
        sent = lax.dynamic_index_in_dim(pieces, 1 - dp_index, axis=1, keepdims=False)
        kept = kept + lax.ppermute(sent, "dp", [(0, 1), (1, 0)])
        grad_w_out = None
        for step in range(side_count):
            perm = []
            for g in range(side_count):
                for h in range(head_count):
                    for p in range(dp_count):
                        owner_side = (g + step) % side_count
                        source = (g * head_count + h) * dp_count + p
                        target = (side_count * h + owner_side) * dp_count + p
                        perm.append((source, target))
            outgoing = lax.dynamic_index_in_dim(
                kept, (side_index + step) % side_count, axis=0, keepdims=False
            )
            arrived = lax.ppermute(outgoing, ALL, perm)
            grad_w_out = arrived if grad_w_out is None else grad_w_out + arrived
    else:
        pieces = partial.reshape(chunk_count, chunk, width)
        holder = side_index * dp_count + dp_index
        grad_w_out = None
        for step in range(chunk_count):
            perm = []
            for g in range(side_count):
                for h in range(head_count):
                    for p in range(dp_count):
                        c = (g * dp_count + p + step) % chunk_count
                        source = (g * head_count + h) * dp_count + p
                        target = (side_count * h + c // dp_count) * dp_count + c % dp_count
                        perm.append((source, target))
            outgoing = lax.dynamic_index_in_dim(
                pieces, (holder + step) % chunk_count, axis=0, keepdims=False
            )
            arrived = lax.ppermute(outgoing, ALL, perm)
            grad_w_out = arrived if grad_w_out is None else grad_w_out + arrived
    return (projected.reshape(1, row_count, width), grad_w_out)


def solution(mesh):
    seq_count = mesh.shape["seq"]
    dp_count = mesh.shape["dp"]
    fine = Mesh(
        mesh.devices.reshape(seq_count // HEADS, HEADS, dp_count), ("side", "inner", "dp")
    )
    seq = ("side", "inner")
    placed = (
        P("dp", seq, None),
        P("dp", seq, None),
        P("dp", seq, None),
        P(ALL, None),
        P("dp", seq, None),
    )
    return jax.shard_map(
        local,
        mesh=fine,
        in_specs=placed,
        out_specs=(P("dp", seq, None), P(ALL, None)),
        check_vma=False,
    )
```

```python
import jax
import jax.numpy as jnp
from jax import lax
from jax.sharding import Mesh
from jax.sharding import PartitionSpec as P

HEADS = 8
HEAD_DIM = 192


def attend(query_here, key_all, value_all):
    query_count = query_here.shape[0]
    head_width = query_here.shape[1]
    block_size = min(512, query_count)
    score_scale = HEAD_DIM ** (-0.5)

    def one_block(query_block):
        scores = jnp.dot(query_block, key_all.T, preferred_element_type=jnp.float32) * score_scale
        largest = jnp.max(scores, axis=1, keepdims=True)
        raised = jnp.exp(scores - largest)
        denominator = jnp.sum(raised, axis=1, keepdims=True)
        weights = raised.astype(jnp.bfloat16)
        mixed = jnp.dot(weights, value_all, preferred_element_type=jnp.float32)
        return (mixed / denominator).astype(jnp.bfloat16)

    blocks = lax.map(
        one_block, query_here.reshape(query_count // block_size, block_size, head_width)
    )
    return blocks.reshape(query_count, head_width)


ALL = ("side", "inner", "dp")


def local(queries, key_vectors, value_vectors, w_out, cotangent):
    head_count = HEADS
    head_width = HEAD_DIM
    side_count = lax.axis_size("side")
    dp_count = lax.axis_size("dp")
    row_count = queries.shape[1]
    width = queries.shape[2]

    dp_index = lax.axis_index("dp")
    w_other = lax.ppermute(w_out, "dp", [(p, (p + 1) % dp_count) for p in range(dp_count)])
    if dp_count == 2:
        w_pair = jnp.stack(
            [jnp.where(dp_index == 0, w_out, w_other), jnp.where(dp_index == 0, w_other, w_out)]
        )
        w_full = lax.all_gather(w_pair, ("side", "inner"), axis=0, tiled=True).reshape(-1, width)
    else:
        w_full = lax.all_gather(w_out, ALL, axis=0, tiled=True)
    cot_side = lax.all_gather(cotangent[0], "inner", axis=0, tiled=True)

    def a2a(tensor):
        return lax.all_to_all(tensor, "inner", split_axis=0, concat_axis=0, tiled=True)

    def by_head(tensor):
        return tensor[0].reshape(row_count, head_count, head_width).transpose(1, 0, 2)

    side_index = lax.axis_index("side")
    kv_raw = jnp.concatenate([by_head(key_vectors), by_head(value_vectors)], axis=2)
    inner_index = lax.axis_index("inner")
    kv_crossed = []
    for step in range(1, side_count):
        for shift in range(head_count):
            perm = [
                (g * head_count + i, ((g + step) % side_count) * head_count + (i + shift) % head_count)
                for g in range(side_count)
                for i in range(head_count)
            ]
            outgoing = lax.dynamic_index_in_dim(
                kv_raw, (inner_index + shift) % head_count, axis=0, keepdims=False
            )
            kv_crossed.append(lax.ppermute(outgoing, ("side", "inner"), perm))
    stacked = jnp.concatenate([by_head(queries), kv_raw], axis=2)
    got = a2a(stacked).reshape(head_count * row_count, 3 * head_width)
    query_here = got[:, :head_width]
    kv_all = jnp.concatenate([got[:, head_width:]] + kv_crossed, axis=0)
    key_all = kv_all[:, :head_width]
    value_all = kv_all[:, head_width:]

    attended_here = attend(query_here, key_all, value_all)

    partial = lax.dot_general(
        attended_here, cot_side, (((0,), (0,)), ((), ())), preferred_element_type=jnp.float32
    )

    returned = a2a(attended_here.reshape(head_count, row_count, head_width))
    attended = returned.transpose(1, 0, 2).reshape(row_count, width)
    projected = jnp.dot(attended, w_full, preferred_element_type=jnp.float32).astype(
        jnp.bfloat16
    )

    chunk_count = side_count * dp_count
    chunk = head_width // chunk_count
    side_index = lax.axis_index("side")
    if dp_count == 2:
        pieces = partial.reshape(side_count, dp_count, chunk, width)
        kept = lax.dynamic_index_in_dim(pieces, dp_index, axis=1, keepdims=False)
        sent = lax.dynamic_index_in_dim(pieces, 1 - dp_index, axis=1, keepdims=False)
        kept = kept + lax.ppermute(sent, "dp", [(0, 1), (1, 0)])
        grad_w_out = None
        for step in range(side_count):
            perm = []
            for g in range(side_count):
                for h in range(head_count):
                    for p in range(dp_count):
                        owner_side = (g + step) % side_count
                        source = (g * head_count + h) * dp_count + p
                        target = (side_count * h + owner_side) * dp_count + p
                        perm.append((source, target))
            outgoing = lax.dynamic_index_in_dim(
                kept, (side_index + step) % side_count, axis=0, keepdims=False
            )
            arrived = lax.ppermute(outgoing, ALL, perm)
            grad_w_out = arrived if grad_w_out is None else grad_w_out + arrived
    else:
        pieces = partial.reshape(chunk_count, chunk, width)
        holder = side_index * dp_count + dp_index
        grad_w_out = None
        for step in range(chunk_count):
            perm = []
            for g in range(side_count):
                for h in range(head_count):
                    for p in range(dp_count):
                        c = (g * dp_count + p + step) % chunk_count
                        source = (g * head_count + h) * dp_count + p
                        target = (side_count * h + c // dp_count) * dp_count + c % dp_count
                        perm.append((source, target))
            outgoing = lax.dynamic_index_in_dim(
                pieces, (holder + step) % chunk_count, axis=0, keepdims=False
            )
            arrived = lax.ppermute(outgoing, ALL, perm)
            grad_w_out = arrived if grad_w_out is None else grad_w_out + arrived
    return (projected.reshape(1, row_count, width), grad_w_out)


def solution(mesh):
    seq_count = mesh.shape["seq"]
    dp_count = mesh.shape["dp"]
    fine = Mesh(
        mesh.devices.reshape(seq_count // HEADS, HEADS, dp_count), ("side", "inner", "dp")
    )
    seq = ("side", "inner")
    placed = (
        P("dp", seq, None),
        P("dp", seq, None),
        P("dp", seq, None),
        P(ALL, None),
        P("dp", seq, None),
    )
    return jax.shard_map(
        local,
        mesh=fine,
        in_specs=placed,
        out_specs=(P("dp", seq, None), P(ALL, None)),
        check_vma=False,
    )
```

```python
import jax
import jax.numpy as jnp
from jax import lax
from jax.sharding import Mesh
from jax.sharding import PartitionSpec as P

HEADS = 8
HEAD_DIM = 192


def attend(query_here, key_all, value_all):
    query_count = query_here.shape[0]
    head_width = query_here.shape[1]
    block_size = min(512, query_count)
    score_scale = HEAD_DIM ** (-0.5)

    def one_block(query_block):
        scores = jnp.dot(query_block, key_all.T, preferred_element_type=jnp.float32) * score_scale
        largest = jnp.max(scores, axis=1, keepdims=True)
        raised = jnp.exp(scores - largest)
        denominator = jnp.sum(raised, axis=1, keepdims=True)
        weights = raised.astype(jnp.bfloat16)
        mixed = jnp.dot(weights, value_all, preferred_element_type=jnp.float32)
        return (mixed / denominator).astype(jnp.bfloat16)

    blocks = lax.map(
        one_block, query_here.reshape(query_count // block_size, block_size, head_width)
    )
    return blocks.reshape(query_count, head_width)


ALL = ("side", "chip", "core", "dp")
INNER = ("chip", "core")
SEQ = ("side", "chip", "core")


def local(queries, key_vectors, value_vectors, w_out, cotangent):
    head_count = HEADS
    head_width = HEAD_DIM
    side_count = lax.axis_size("side")
    dp_count = lax.axis_size("dp")
    row_count = queries.shape[1]
    width = queries.shape[2]

    dp_index = lax.axis_index("dp")
    chip_count = lax.axis_size("chip")
    core_count = lax.axis_size("core")
    core_index = lax.axis_index("core")
    if dp_count == 2:
        w_other = lax.ppermute(w_out, "dp", [(0, 1), (1, 0)])
        w_pair = jnp.stack(
            [jnp.where(dp_index == 0, w_out, w_other), jnp.where(dp_index == 0, w_other, w_out)]
        )
        w_core = lax.all_gather(w_pair, ("side", "chip"), axis=0, tiled=True).reshape(-1, width)
    else:
        w_core = lax.all_gather(w_out, ("side", "chip", "dp"), axis=0, tiled=True)
    w_partner = lax.ppermute(w_core, "core", [(0, 1), (1, 0)])
    cot_side = lax.all_gather(cotangent[0], INNER, axis=0, tiled=True)

    def a2a(tensor):
        return lax.all_to_all(tensor, INNER, split_axis=0, concat_axis=0, tiled=True)

    def by_head(tensor):
        return tensor[0].reshape(row_count, head_count, head_width).transpose(1, 0, 2)

    side_index = lax.axis_index("side")
    kv_raw = jnp.concatenate([by_head(key_vectors), by_head(value_vectors)], axis=2)
    inner_index = lax.axis_index("chip") * core_count + core_index
    kv_crossed = []
    for step in range(1, side_count):
        for shift in range(head_count):
            perm = [
                (g * head_count + i, ((g + step) % side_count) * head_count + (i + shift) % head_count)
                for g in range(side_count)
                for i in range(head_count)
            ]
            outgoing = lax.dynamic_index_in_dim(
                kv_raw, (inner_index + shift) % head_count, axis=0, keepdims=False
            )
            kv_crossed.append(lax.ppermute(outgoing, SEQ, perm))
    stacked = jnp.concatenate([by_head(queries), kv_raw], axis=2)
    got = a2a(stacked).reshape(head_count * row_count, 3 * head_width)
    query_here = got[:, :head_width]
    kv_all = jnp.concatenate([got[:, head_width:]] + kv_crossed, axis=0)
    key_all = kv_all[:, :head_width]
    value_all = kv_all[:, head_width:]

    attended_here = attend(query_here, key_all, value_all)
    w_partner, attended_here = lax.optimization_barrier((w_partner, attended_here))

    partial = lax.dot_general(
        attended_here, cot_side, (((0,), (0,)), ((), ())), preferred_element_type=jnp.float32
    )

    returned = a2a(attended_here.reshape(head_count, row_count, head_width))
    attended = returned.transpose(1, 0, 2).reshape(row_count, width)
    by_core = attended.reshape(row_count, side_count * chip_count, core_count, -1)
    mine = lax.dynamic_index_in_dim(by_core, core_index, axis=2, keepdims=False)
    theirs = lax.dynamic_index_in_dim(by_core, 1 - core_index, axis=2, keepdims=False)
    projected = (
        jnp.dot(mine.reshape(row_count, -1), w_core, preferred_element_type=jnp.float32)
        + jnp.dot(theirs.reshape(row_count, -1), w_partner, preferred_element_type=jnp.float32)
    ).astype(jnp.bfloat16)

    chunk_count = side_count * dp_count
    chunk = head_width // chunk_count
    side_index = lax.axis_index("side")
    if dp_count == 2:
        pieces = partial.reshape(side_count, dp_count, chunk, width)
        kept = lax.dynamic_index_in_dim(pieces, dp_index, axis=1, keepdims=False)
        sent = lax.dynamic_index_in_dim(pieces, 1 - dp_index, axis=1, keepdims=False)
        kept = kept + lax.ppermute(sent, "dp", [(0, 1), (1, 0)])
        grad_w_out = None
        for step in range(side_count):
            perm = []
            for g in range(side_count):
                for h in range(head_count):
                    for p in range(dp_count):
                        owner_side = (g + step) % side_count
                        source = (g * head_count + h) * dp_count + p
                        target = (side_count * h + owner_side) * dp_count + p
                        perm.append((source, target))
            outgoing = lax.dynamic_index_in_dim(
                kept, (side_index + step) % side_count, axis=0, keepdims=False
            )
            arrived = lax.ppermute(outgoing, ALL, perm)
            grad_w_out = arrived if grad_w_out is None else grad_w_out + arrived
    else:
        pieces = partial.reshape(chunk_count, chunk, width)
        holder = side_index * dp_count + dp_index
        grad_w_out = None
        for step in range(chunk_count):
            perm = []
            for g in range(side_count):
                for h in range(head_count):
                    for p in range(dp_count):
                        c = (g * dp_count + p + step) % chunk_count
                        source = (g * head_count + h) * dp_count + p
                        target = (side_count * h + c // dp_count) * dp_count + c % dp_count
                        perm.append((source, target))
            outgoing = lax.dynamic_index_in_dim(
                pieces, (holder + step) % chunk_count, axis=0, keepdims=False
            )
            arrived = lax.ppermute(outgoing, ALL, perm)
            grad_w_out = arrived if grad_w_out is None else grad_w_out + arrived
    return (projected.reshape(1, row_count, width), grad_w_out)


def solution(mesh):
    seq_count = mesh.shape["seq"]
    dp_count = mesh.shape["dp"]
    fine = Mesh(mesh.devices.reshape(seq_count // HEADS, HEADS // 2, 2, dp_count), ALL)
    seq = SEQ
    placed = (
        P("dp", seq, None),
        P("dp", seq, None),
        P("dp", seq, None),
        P(ALL, None),
        P("dp", seq, None),
    )
    return jax.shard_map(
        local,
        mesh=fine,
        in_specs=placed,
        out_specs=(P("dp", seq, None), P(ALL, None)),
        check_vma=False,
    )
```

```python
import jax
import jax.numpy as jnp
from jax import lax
from jax.sharding import Mesh
from jax.sharding import PartitionSpec as P

HEADS = 8
HEAD_DIM = 192


def attend_part(query_here, key_part, value_part):
    query_count = query_here.shape[0]
    head_width = query_here.shape[1]
    block_size = min(512, query_count)
    score_scale = HEAD_DIM ** (-0.5)

    def one_block(query_block):
        scores = jnp.dot(query_block, key_part.T, preferred_element_type=jnp.float32) * score_scale
        largest = jnp.max(scores, axis=1, keepdims=True)
        raised = jnp.exp(scores - largest)
        denominator = jnp.sum(raised, axis=1, keepdims=True)
        weights = raised.astype(jnp.bfloat16)
        mixed = jnp.dot(weights, value_part, preferred_element_type=jnp.float32)
        return mixed, largest, denominator

    mixed, largest, denominator = lax.map(
        one_block, query_here.reshape(query_count // block_size, block_size, head_width)
    )
    return (
        mixed.reshape(query_count, -1),
        largest.reshape(query_count, 1),
        denominator.reshape(query_count, 1),
    )


def combine(results):
    largest = results[0][1]
    for _, part_largest, _ in results[1:]:
        largest = jnp.maximum(largest, part_largest)
    mixed = 0.0
    denominator = 0.0
    for part_mixed, part_largest, part_denominator in results:
        scale = jnp.exp(part_largest - largest)
        mixed = mixed + part_mixed * scale
        denominator = denominator + part_denominator * scale
    return (mixed / denominator).astype(jnp.bfloat16)


ALL = ("side", "inner", "dp")


def local(queries, key_vectors, value_vectors, w_out, cotangent):
    head_count = HEADS
    head_width = HEAD_DIM
    side_count = lax.axis_size("side")
    dp_count = lax.axis_size("dp")
    row_count = queries.shape[1]
    width = queries.shape[2]

    dp_index = lax.axis_index("dp")
    w_other = lax.ppermute(w_out, "dp", [(p, (p + 1) % dp_count) for p in range(dp_count)])
    if dp_count == 2:
        w_pair = jnp.stack(
            [jnp.where(dp_index == 0, w_out, w_other), jnp.where(dp_index == 0, w_other, w_out)]
        )
        w_full = lax.all_gather(w_pair, ("side", "inner"), axis=0, tiled=True).reshape(-1, width)
    else:
        w_full = lax.all_gather(w_out, ALL, axis=0, tiled=True)
    cot_side = lax.all_gather(cotangent[0], "inner", axis=0, tiled=True)

    def a2a(tensor):
        return lax.all_to_all(tensor, "inner", split_axis=0, concat_axis=0, tiled=True)

    def by_head(tensor):
        return tensor[0].reshape(row_count, head_count, head_width).transpose(1, 0, 2)

    side_index = lax.axis_index("side")
    kv_raw = jnp.concatenate([by_head(key_vectors), by_head(value_vectors)], axis=2)
    inner_index = lax.axis_index("inner")
    kv_crossed = []
    for step in range(1, side_count):
        for shift in range(head_count):
            perm = [
                (g * head_count + i, ((g + step) % side_count) * head_count + (i + shift) % head_count)
                for g in range(side_count)
                for i in range(head_count)
            ]
            outgoing = lax.dynamic_index_in_dim(
                kv_raw, (inner_index + shift) % head_count, axis=0, keepdims=False
            )
            kv_crossed.append(lax.ppermute(outgoing, ("side", "inner"), perm))
    stacked = jnp.concatenate([by_head(queries), kv_raw], axis=2)
    got = a2a(stacked).reshape(head_count * row_count, 3 * head_width)
    query_here = got[:, :head_width]
    kv_here = got[:, head_width:]
    near = attend_part(query_here, kv_here[:, :head_width], kv_here[:, head_width:])
    kv_crossed, near = lax.optimization_barrier((kv_crossed, near))
    kv_there = jnp.concatenate(kv_crossed, axis=0)
    far = attend_part(query_here, kv_there[:, :head_width], kv_there[:, head_width:])

    attended_here = combine([near, far])

    partial = lax.dot_general(
        attended_here, cot_side, (((0,), (0,)), ((), ())), preferred_element_type=jnp.float32
    )

    returned = a2a(attended_here.reshape(head_count, row_count, head_width))
    attended = returned.transpose(1, 0, 2).reshape(row_count, width)
    projected = jnp.dot(attended, w_full, preferred_element_type=jnp.float32).astype(
        jnp.bfloat16
    )

    chunk_count = side_count * dp_count
    chunk = head_width // chunk_count
    side_index = lax.axis_index("side")
    if dp_count == 2:
        pieces = partial.reshape(side_count, dp_count, chunk, width)
        kept = lax.dynamic_index_in_dim(pieces, dp_index, axis=1, keepdims=False)
        sent = lax.dynamic_index_in_dim(pieces, 1 - dp_index, axis=1, keepdims=False)
        kept = kept + lax.ppermute(sent, "dp", [(0, 1), (1, 0)])
        grad_w_out = None
        for step in range(side_count):
            perm = []
            for g in range(side_count):
                for h in range(head_count):
                    for p in range(dp_count):
                        owner_side = (g + step) % side_count
                        source = (g * head_count + h) * dp_count + p
                        target = (side_count * h + owner_side) * dp_count + p
                        perm.append((source, target))
            outgoing = lax.dynamic_index_in_dim(
                kept, (side_index + step) % side_count, axis=0, keepdims=False
            )
            arrived = lax.ppermute(outgoing, ALL, perm)
            grad_w_out = arrived if grad_w_out is None else grad_w_out + arrived
    else:
        pieces = partial.reshape(chunk_count, chunk, width)
        holder = side_index * dp_count + dp_index
        grad_w_out = None
        for step in range(chunk_count):
            perm = []
            for g in range(side_count):
                for h in range(head_count):
                    for p in range(dp_count):
                        c = (g * dp_count + p + step) % chunk_count
                        source = (g * head_count + h) * dp_count + p
                        target = (side_count * h + c // dp_count) * dp_count + c % dp_count
                        perm.append((source, target))
            outgoing = lax.dynamic_index_in_dim(
                pieces, (holder + step) % chunk_count, axis=0, keepdims=False
            )
            arrived = lax.ppermute(outgoing, ALL, perm)
            grad_w_out = arrived if grad_w_out is None else grad_w_out + arrived
    return (projected.reshape(1, row_count, width), grad_w_out)


def solution(mesh):
    seq_count = mesh.shape["seq"]
    dp_count = mesh.shape["dp"]
    fine = Mesh(
        mesh.devices.reshape(seq_count // HEADS, HEADS, dp_count), ("side", "inner", "dp")
    )
    seq = ("side", "inner")
    placed = (
        P("dp", seq, None),
        P("dp", seq, None),
        P("dp", seq, None),
        P(ALL, None),
        P("dp", seq, None),
    )
    return jax.shard_map(
        local,
        mesh=fine,
        in_specs=placed,
        out_specs=(P("dp", seq, None), P(ALL, None)),
        check_vma=False,
    )
```

```python
import jax
import jax.numpy as jnp
from jax import lax
from jax.sharding import Mesh
from jax.sharding import PartitionSpec as P

HEADS = 8
HEAD_DIM = 192


def attend(query_here, key_all, value_all):
    query_count = query_here.shape[0]
    head_width = query_here.shape[1]
    block_size = min(512, query_count)
    score_scale = HEAD_DIM ** (-0.5)

    def one_block(query_block):
        scores = jnp.dot(query_block, key_all.T, preferred_element_type=jnp.float32) * score_scale
        largest = jnp.max(scores, axis=1, keepdims=True)
        raised = jnp.exp(scores - largest)
        denominator = jnp.sum(raised, axis=1, keepdims=True)
        weights = raised.astype(jnp.bfloat16)
        mixed = jnp.dot(weights, value_all, preferred_element_type=jnp.float32)
        return (mixed / denominator).astype(jnp.bfloat16)

    blocks = lax.map(
        one_block, query_here.reshape(query_count // block_size, block_size, head_width)
    )
    return blocks.reshape(query_count, head_width)


ALL = ("side", "inner", "dp")


def local(queries, key_vectors, value_vectors, w_out, cotangent):
    head_count = HEADS
    head_width = HEAD_DIM
    side_count = lax.axis_size("side")
    dp_count = lax.axis_size("dp")
    row_count = queries.shape[1]
    width = queries.shape[2]

    dp_index = lax.axis_index("dp")
    w_full = lax.all_gather(w_out, ALL, axis=0, tiled=True)
    cot_side = lax.all_gather(cotangent[0], "inner", axis=0, tiled=True)

    def a2a(tensor):
        return lax.all_to_all(tensor, "inner", split_axis=0, concat_axis=0, tiled=True)

    def by_head(tensor):
        return tensor[0].reshape(row_count, head_count, head_width).transpose(1, 0, 2)

    side_index = lax.axis_index("side")
    kv_raw = jnp.concatenate([by_head(key_vectors), by_head(value_vectors)], axis=2)
    inner_index = lax.axis_index("inner")
    kv_crossed = []
    for step in range(1, side_count):
        for shift in range(head_count):
            perm = [
                (g * head_count + i, ((g + step) % side_count) * head_count + (i + shift) % head_count)
                for g in range(side_count)
                for i in range(head_count)
            ]
            outgoing = lax.dynamic_index_in_dim(
                kv_raw, (inner_index + shift) % head_count, axis=0, keepdims=False
            )
            kv_crossed.append(lax.ppermute(outgoing, ("side", "inner"), perm))
    stacked = jnp.concatenate([by_head(queries), kv_raw], axis=2)
    got = a2a(stacked).reshape(head_count * row_count, 3 * head_width)
    query_here = got[:, :head_width]
    kv_all = jnp.concatenate([got[:, head_width:]] + kv_crossed, axis=0)
    key_all = kv_all[:, :head_width]
    value_all = kv_all[:, head_width:]

    attended_here = attend(query_here, key_all, value_all)

    partial = lax.dot_general(
        attended_here, cot_side, (((0,), (0,)), ((), ())), preferred_element_type=jnp.float32
    )

    returned = a2a(attended_here.reshape(head_count, row_count, head_width))
    attended = returned.transpose(1, 0, 2).reshape(row_count, width)
    projected = jnp.dot(attended, w_full, preferred_element_type=jnp.float32).astype(
        jnp.bfloat16
    )

    chunk_count = side_count * dp_count
    chunk = head_width // chunk_count
    side_index = lax.axis_index("side")
    if dp_count == 2:
        pieces = partial.reshape(side_count, dp_count, chunk, width)
        kept = lax.dynamic_index_in_dim(pieces, dp_index, axis=1, keepdims=False)
        sent = lax.dynamic_index_in_dim(pieces, 1 - dp_index, axis=1, keepdims=False)
        kept = kept + lax.ppermute(sent, "dp", [(0, 1), (1, 0)])
        grad_w_out = None
        for step in range(side_count):
            perm = []
            for g in range(side_count):
                for h in range(head_count):
                    for p in range(dp_count):
                        owner_side = (g + step) % side_count
                        source = (g * head_count + h) * dp_count + p
                        target = (side_count * h + owner_side) * dp_count + p
                        perm.append((source, target))
            outgoing = lax.dynamic_index_in_dim(
                kept, (side_index + step) % side_count, axis=0, keepdims=False
            )
            arrived = lax.ppermute(outgoing, ALL, perm)
            grad_w_out = arrived if grad_w_out is None else grad_w_out + arrived
    else:
        pieces = partial.reshape(chunk_count, chunk, width)
        holder = side_index * dp_count + dp_index
        grad_w_out = None
        for step in range(chunk_count):
            perm = []
            for g in range(side_count):
                for h in range(head_count):
                    for p in range(dp_count):
                        c = (g * dp_count + p + step) % chunk_count
                        source = (g * head_count + h) * dp_count + p
                        target = (side_count * h + c // dp_count) * dp_count + c % dp_count
                        perm.append((source, target))
            outgoing = lax.dynamic_index_in_dim(
                pieces, (holder + step) % chunk_count, axis=0, keepdims=False
            )
            arrived = lax.ppermute(outgoing, ALL, perm)
            grad_w_out = arrived if grad_w_out is None else grad_w_out + arrived
    return (projected.reshape(1, row_count, width), grad_w_out)


def solution(mesh):
    seq_count = mesh.shape["seq"]
    dp_count = mesh.shape["dp"]
    fine = Mesh(
        mesh.devices.reshape(seq_count // HEADS, HEADS, dp_count), ("side", "inner", "dp")
    )
    seq = ("side", "inner")
    placed = (
        P("dp", seq, None),
        P("dp", seq, None),
        P("dp", seq, None),
        P(ALL, None),
        P("dp", seq, None),
    )
    return jax.shard_map(
        local,
        mesh=fine,
        in_specs=placed,
        out_specs=(P("dp", seq, None), P(ALL, None)),
        check_vma=False,
    )
```

```python
import jax
import jax.numpy as jnp
from jax import lax
from jax.sharding import Mesh
from jax.sharding import PartitionSpec as P

HEADS = 8
HEAD_DIM = 192


def attend(query_here, key_all, value_all):
    query_count = query_here.shape[0]
    head_width = query_here.shape[1]
    block_size = min(512, query_count)
    score_scale = HEAD_DIM ** (-0.5)

    def one_block(query_block):
        scores = jnp.dot(query_block, key_all.T, preferred_element_type=jnp.float32) * score_scale
        largest = jnp.max(scores, axis=1, keepdims=True)
        raised = jnp.exp(scores - largest)
        denominator = jnp.sum(raised, axis=1, keepdims=True)
        weights = raised.astype(jnp.bfloat16)
        mixed = jnp.dot(weights, value_all, preferred_element_type=jnp.float32)
        return (mixed / denominator).astype(jnp.bfloat16)

    blocks = lax.map(
        one_block, query_here.reshape(query_count // block_size, block_size, head_width)
    )
    return blocks.reshape(query_count, head_width)


ALL = ("side", "inner", "dp")


def local(queries, key_vectors, value_vectors, w_out, cotangent):
    head_count = HEADS
    head_width = HEAD_DIM
    side_count = lax.axis_size("side")
    dp_count = lax.axis_size("dp")
    row_count = queries.shape[1]
    width = queries.shape[2]

    dp_index = lax.axis_index("dp")
    w_full = lax.all_gather(w_out, ALL, axis=0, tiled=True)
    cot_side = lax.all_gather(cotangent[0], "inner", axis=0, tiled=True)

    def a2a(tensor):
        return lax.all_to_all(tensor, "inner", split_axis=0, concat_axis=0, tiled=True)

    def by_head(tensor):
        return tensor[0].reshape(row_count, head_count, head_width).transpose(1, 0, 2)

    side_index = lax.axis_index("side")
    kv_raw = jnp.concatenate([by_head(key_vectors), by_head(value_vectors)], axis=2)
    inner_index = lax.axis_index("inner")
    chip_count = head_count // 2
    chip_index = inner_index // 2
    parity = inner_index % 2
    by_chip = kv_raw.reshape(chip_count, 2, row_count, 2 * head_width)
    seq_count = side_count * head_count
    kv_crossed = []
    for step in range(1, side_count):
        own_pieces = []
        partner_pieces = []
        for shift in range(chip_count):
            perm = [
                (
                    g * head_count + 2 * c + k,
                    ((g + step) % side_count) * head_count + 2 * ((c + shift) % chip_count) + k,
                )
                for g in range(side_count)
                for c in range(chip_count)
                for k in range(2)
            ]
            outgoing = lax.dynamic_index_in_dim(
                by_chip, (chip_index + shift) % chip_count, axis=0, keepdims=False
            )
            arrived = lax.ppermute(outgoing, ("side", "inner"), perm)
            own_pieces.append(lax.dynamic_index_in_dim(arrived, parity, axis=0, keepdims=False))
            partner_pieces.append(
                lax.dynamic_index_in_dim(arrived, 1 - parity, axis=0, keepdims=False)
            )
        swapped = lax.ppermute(
            jnp.stack(partner_pieces), ("side", "inner"), [(s, s ^ 1) for s in range(seq_count)]
        )
        kv_crossed.append(jnp.stack(own_pieces).reshape(-1, 2 * head_width))
        kv_crossed.append(swapped.reshape(-1, 2 * head_width))
    stacked = jnp.concatenate([by_head(queries), kv_raw], axis=2)
    got = a2a(stacked).reshape(head_count * row_count, 3 * head_width)
    query_here = got[:, :head_width]
    kv_all = jnp.concatenate([got[:, head_width:]] + kv_crossed, axis=0)
    key_all = kv_all[:, :head_width]
    value_all = kv_all[:, head_width:]

    attended_here = attend(query_here, key_all, value_all)

    partial = lax.dot_general(
        attended_here, cot_side, (((0,), (0,)), ((), ())), preferred_element_type=jnp.float32
    )

    returned = a2a(attended_here.reshape(head_count, row_count, head_width))
    attended = returned.transpose(1, 0, 2).reshape(row_count, width)
    projected = jnp.dot(attended, w_full, preferred_element_type=jnp.float32).astype(
        jnp.bfloat16
    )

    chunk_count = side_count * dp_count
    chunk = head_width // chunk_count
    side_index = lax.axis_index("side")
    if dp_count == 2:
        pieces = partial.reshape(side_count, dp_count, chunk, width)
        kept = lax.dynamic_index_in_dim(pieces, dp_index, axis=1, keepdims=False)
        sent = lax.dynamic_index_in_dim(pieces, 1 - dp_index, axis=1, keepdims=False)
        kept = kept + lax.ppermute(sent, "dp", [(0, 1), (1, 0)])
        grad_w_out = None
        for step in range(side_count):
            perm = []
            for g in range(side_count):
                for h in range(head_count):
                    for p in range(dp_count):
                        owner_side = (g + step) % side_count
                        source = (g * head_count + h) * dp_count + p
                        target = (side_count * h + owner_side) * dp_count + p
                        perm.append((source, target))
            outgoing = lax.dynamic_index_in_dim(
                kept, (side_index + step) % side_count, axis=0, keepdims=False
            )
            arrived = lax.ppermute(outgoing, ALL, perm)
            grad_w_out = arrived if grad_w_out is None else grad_w_out + arrived
    else:
        pieces = partial.reshape(chunk_count, chunk, width)
        holder = side_index * dp_count + dp_index
        grad_w_out = None
        for step in range(chunk_count):
            perm = []
            for g in range(side_count):
                for h in range(head_count):
                    for p in range(dp_count):
                        c = (g * dp_count + p + step) % chunk_count
                        source = (g * head_count + h) * dp_count + p
                        target = (side_count * h + c // dp_count) * dp_count + c % dp_count
                        perm.append((source, target))
            outgoing = lax.dynamic_index_in_dim(
                pieces, (holder + step) % chunk_count, axis=0, keepdims=False
            )
            arrived = lax.ppermute(outgoing, ALL, perm)
            grad_w_out = arrived if grad_w_out is None else grad_w_out + arrived
    return (projected.reshape(1, row_count, width), grad_w_out)


def solution(mesh):
    seq_count = mesh.shape["seq"]
    dp_count = mesh.shape["dp"]
    fine = Mesh(
        mesh.devices.reshape(seq_count // HEADS, HEADS, dp_count), ("side", "inner", "dp")
    )
    seq = ("side", "inner")
    placed = (
        P("dp", seq, None),
        P("dp", seq, None),
        P("dp", seq, None),
        P(ALL, None),
        P("dp", seq, None),
    )
    return jax.shard_map(
        local,
        mesh=fine,
        in_specs=placed,
        out_specs=(P("dp", seq, None), P(ALL, None)),
        check_vma=False,
    )
```

```python
import jax
import jax.numpy as jnp
from jax import lax
from jax.sharding import Mesh
from jax.sharding import PartitionSpec as P

HEADS = 8
HEAD_DIM = 192


def attend(query_here, key_all, value_all):
    query_count = query_here.shape[0]
    head_width = query_here.shape[1]
    block_size = min(768, query_count)
    score_scale = HEAD_DIM ** (-0.5)

    def one_block(query_block):
        scores = jnp.dot(query_block, key_all.T, preferred_element_type=jnp.float32) * score_scale
        largest = jnp.max(scores, axis=1, keepdims=True)
        raised = jnp.exp(scores - largest)
        denominator = jnp.sum(raised, axis=1, keepdims=True)
        weights = raised.astype(jnp.bfloat16)
        mixed = jnp.dot(weights, value_all, preferred_element_type=jnp.float32)
        return (mixed / denominator).astype(jnp.bfloat16)

    blocks = lax.map(
        one_block, query_here.reshape(query_count // block_size, block_size, head_width)
    )
    return blocks.reshape(query_count, head_width)


ALL = ("side", "inner", "dp")


def local(queries, key_vectors, value_vectors, w_out, cotangent):
    head_count = HEADS
    head_width = HEAD_DIM
    side_count = lax.axis_size("side")
    dp_count = lax.axis_size("dp")
    row_count = queries.shape[1]
    width = queries.shape[2]

    dp_index = lax.axis_index("dp")
    w_full = lax.all_gather(w_out, ALL, axis=0, tiled=True)
    cot_side = lax.all_gather(cotangent[0], "inner", axis=0, tiled=True)

    def a2a(tensor):
        return lax.all_to_all(tensor, "inner", split_axis=0, concat_axis=0, tiled=True)

    def by_head(tensor):
        return tensor[0].reshape(row_count, head_count, head_width).transpose(1, 0, 2)

    side_index = lax.axis_index("side")
    kv_raw = jnp.concatenate([by_head(key_vectors), by_head(value_vectors)], axis=2)
    inner_index = lax.axis_index("inner")
    kv_crossed = []
    for step in range(1, side_count):
        for shift in range(head_count):
            perm = [
                (g * head_count + i, ((g + step) % side_count) * head_count + (i + shift) % head_count)
                for g in range(side_count)
                for i in range(head_count)
            ]
            outgoing = lax.dynamic_index_in_dim(
                kv_raw, (inner_index + shift) % head_count, axis=0, keepdims=False
            )
            kv_crossed.append(lax.ppermute(outgoing, ("side", "inner"), perm))
    stacked = jnp.concatenate([by_head(queries), kv_raw], axis=2)
    got = a2a(stacked).reshape(head_count * row_count, 3 * head_width)
    query_here = got[:, :head_width]
    kv_all = jnp.concatenate([got[:, head_width:]] + kv_crossed, axis=0)
    key_all = kv_all[:, :head_width]
    value_all = kv_all[:, head_width:]

    attended_here = attend(query_here, key_all, value_all)

    partial = lax.dot_general(
        attended_here, cot_side, (((0,), (0,)), ((), ())), preferred_element_type=jnp.float32
    )

    returned = a2a(attended_here.reshape(head_count, row_count, head_width))
    attended = returned.transpose(1, 0, 2).reshape(row_count, width)
    projected = jnp.dot(attended, w_full, preferred_element_type=jnp.float32).astype(
        jnp.bfloat16
    )

    chunk_count = side_count * dp_count
    chunk = head_width // chunk_count
    side_index = lax.axis_index("side")
    if dp_count == 2:
        pieces = partial.reshape(side_count, dp_count, chunk, width)
        kept = lax.dynamic_index_in_dim(pieces, dp_index, axis=1, keepdims=False)
        sent = lax.dynamic_index_in_dim(pieces, 1 - dp_index, axis=1, keepdims=False)
        kept = kept + lax.ppermute(sent, "dp", [(0, 1), (1, 0)])
        grad_w_out = None
        for step in range(side_count):
            perm = []
            for g in range(side_count):
                for h in range(head_count):
                    for p in range(dp_count):
                        owner_side = (g + step) % side_count
                        source = (g * head_count + h) * dp_count + p
                        target = (side_count * h + owner_side) * dp_count + p
                        perm.append((source, target))
            outgoing = lax.dynamic_index_in_dim(
                kept, (side_index + step) % side_count, axis=0, keepdims=False
            )
            arrived = lax.ppermute(outgoing, ALL, perm)
            grad_w_out = arrived if grad_w_out is None else grad_w_out + arrived
    else:
        pieces = partial.reshape(chunk_count, chunk, width)
        holder = side_index * dp_count + dp_index
        grad_w_out = None
        for step in range(chunk_count):
            perm = []
            for g in range(side_count):
                for h in range(head_count):
                    for p in range(dp_count):
                        c = (g * dp_count + p + step) % chunk_count
                        source = (g * head_count + h) * dp_count + p
                        target = (side_count * h + c // dp_count) * dp_count + c % dp_count
                        perm.append((source, target))
            outgoing = lax.dynamic_index_in_dim(
                pieces, (holder + step) % chunk_count, axis=0, keepdims=False
            )
            arrived = lax.ppermute(outgoing, ALL, perm)
            grad_w_out = arrived if grad_w_out is None else grad_w_out + arrived
    return (projected.reshape(1, row_count, width), grad_w_out)


def solution(mesh):
    seq_count = mesh.shape["seq"]
    dp_count = mesh.shape["dp"]
    fine = Mesh(
        mesh.devices.reshape(seq_count // HEADS, HEADS, dp_count), ("side", "inner", "dp")
    )
    seq = ("side", "inner")
    placed = (
        P("dp", seq, None),
        P("dp", seq, None),
        P("dp", seq, None),
        P(ALL, None),
        P("dp", seq, None),
    )
    return jax.shard_map(
        local,
        mesh=fine,
        in_specs=placed,
        out_specs=(P("dp", seq, None), P(ALL, None)),
        check_vma=False,
    )
```

```python
import jax
import jax.numpy as jnp
from jax import lax
from jax.sharding import Mesh
from jax.sharding import PartitionSpec as P

HEADS = 8
HEAD_DIM = 192


def attend(query_here, key_all, value_all):
    query_count = query_here.shape[0]
    head_width = query_here.shape[1]
    block_size = min(512, query_count)
    score_scale = HEAD_DIM ** (-0.5)

    def one_block(query_block):
        scores = jnp.dot(query_block, key_all.T, preferred_element_type=jnp.float32) * score_scale
        largest = jnp.max(scores, axis=1, keepdims=True)
        raised = jnp.exp(scores - largest)
        denominator = jnp.sum(raised, axis=1, keepdims=True)
        weights = raised.astype(jnp.bfloat16)
        mixed = jnp.dot(weights, value_all, preferred_element_type=jnp.float32)
        return (mixed / denominator).astype(jnp.bfloat16)

    blocks = lax.map(
        one_block, query_here.reshape(query_count // block_size, block_size, head_width)
    )
    return blocks.reshape(query_count, head_width)


ALL = ("side", "chip", "core", "dp")
INNER = ("chip", "core")
SEQ = ("side", "chip", "core")


def local(queries, key_vectors, value_vectors, w_out, cotangent):
    head_count = HEADS
    head_width = HEAD_DIM
    side_count = lax.axis_size("side")
    dp_count = lax.axis_size("dp")
    row_count = queries.shape[1]
    width = queries.shape[2]

    dp_index = lax.axis_index("dp")
    chip_count = lax.axis_size("chip")
    core_count = lax.axis_size("core")
    core_index = lax.axis_index("core")
    w_full = lax.all_gather(w_out, ALL, axis=0, tiled=True)
    cot_core = lax.all_gather(cotangent[0], "chip", axis=0, tiled=True)
    cot_other = lax.ppermute(cot_core, "core", [(0, 1), (1, 0)])
    cot_side = jnp.concatenate(
        [
            jnp.where(core_index == 0, cot_core, cot_other),
            jnp.where(core_index == 0, cot_other, cot_core),
        ],
        axis=0,
    )

    def a2a(tensor):
        return lax.all_to_all(tensor, INNER, split_axis=0, concat_axis=0, tiled=True)

    def by_head(tensor):
        return tensor[0].reshape(row_count, head_count, head_width).transpose(1, 0, 2)

    side_index = lax.axis_index("side")
    kv_raw = jnp.concatenate([by_head(key_vectors), by_head(value_vectors)], axis=2)
    inner_index = lax.axis_index("chip") * core_count + core_index
    kv_crossed = []
    for step in range(1, side_count):
        for shift in range(head_count):
            perm = [
                (g * head_count + i, ((g + step) % side_count) * head_count + (i + shift) % head_count)
                for g in range(side_count)
                for i in range(head_count)
            ]
            outgoing = lax.dynamic_index_in_dim(
                kv_raw, (inner_index + shift) % head_count, axis=0, keepdims=False
            )
            kv_crossed.append(lax.ppermute(outgoing, SEQ, perm))
    stacked = jnp.concatenate([by_head(queries), kv_raw], axis=2)
    got = a2a(stacked).reshape(head_count * row_count, 3 * head_width)
    query_here = got[:, :head_width]
    kv_all = jnp.concatenate([got[:, head_width:]] + kv_crossed, axis=0)
    key_all = kv_all[:, :head_width]
    value_all = kv_all[:, head_width:]

    attended_here = attend(query_here, key_all, value_all)

    attended_rows = (
        attended_here.reshape(chip_count, core_count, row_count, head_width)
        .transpose(1, 0, 2, 3)
        .reshape(core_count * chip_count * row_count, head_width)
    )
    partial = lax.dot_general(
        attended_rows, cot_side, (((0,), (0,)), ((), ())), preferred_element_type=jnp.float32
    )

    returned = a2a(attended_here.reshape(head_count, row_count, head_width))
    attended = returned.transpose(1, 0, 2).reshape(row_count, width)
    projected = jnp.dot(attended, w_full, preferred_element_type=jnp.float32).astype(
        jnp.bfloat16
    )

    chunk_count = side_count * dp_count
    chunk = head_width // chunk_count
    side_index = lax.axis_index("side")
    if dp_count == 2:
        pieces = partial.reshape(side_count, dp_count, chunk, width)
        kept = lax.dynamic_index_in_dim(pieces, dp_index, axis=1, keepdims=False)
        sent = lax.dynamic_index_in_dim(pieces, 1 - dp_index, axis=1, keepdims=False)
        kept = kept + lax.ppermute(sent, "dp", [(0, 1), (1, 0)])
        grad_w_out = None
        for step in range(side_count):
            perm = []
            for g in range(side_count):
                for h in range(head_count):
                    for p in range(dp_count):
                        owner_side = (g + step) % side_count
                        source = (g * head_count + h) * dp_count + p
                        target = (side_count * h + owner_side) * dp_count + p
                        perm.append((source, target))
            outgoing = lax.dynamic_index_in_dim(
                kept, (side_index + step) % side_count, axis=0, keepdims=False
            )
            arrived = lax.ppermute(outgoing, ALL, perm)
            grad_w_out = arrived if grad_w_out is None else grad_w_out + arrived
    else:
        pieces = partial.reshape(chunk_count, chunk, width)
        holder = side_index * dp_count + dp_index
        grad_w_out = None
        for step in range(chunk_count):
            perm = []
            for g in range(side_count):
                for h in range(head_count):
                    for p in range(dp_count):
                        c = (g * dp_count + p + step) % chunk_count
                        source = (g * head_count + h) * dp_count + p
                        target = (side_count * h + c // dp_count) * dp_count + c % dp_count
                        perm.append((source, target))
            outgoing = lax.dynamic_index_in_dim(
                pieces, (holder + step) % chunk_count, axis=0, keepdims=False
            )
            arrived = lax.ppermute(outgoing, ALL, perm)
            grad_w_out = arrived if grad_w_out is None else grad_w_out + arrived
    return (projected.reshape(1, row_count, width), grad_w_out)


def solution(mesh):
    seq_count = mesh.shape["seq"]
    dp_count = mesh.shape["dp"]
    fine = Mesh(mesh.devices.reshape(seq_count // HEADS, HEADS // 2, 2, dp_count), ALL)
    seq = SEQ
    placed = (
        P("dp", seq, None),
        P("dp", seq, None),
        P("dp", seq, None),
        P(ALL, None),
        P("dp", seq, None),
    )
    return jax.shard_map(
        local,
        mesh=fine,
        in_specs=placed,
        out_specs=(P("dp", seq, None), P(ALL, None)),
        check_vma=False,
    )
```

```python
import jax
import jax.numpy as jnp
from jax import lax
from jax.sharding import Mesh
from jax.sharding import PartitionSpec as P

HEADS = 8
HEAD_DIM = 192


def attend(query_here, key_all, value_all):
    query_count = query_here.shape[0]
    head_width = query_here.shape[1]
    block_size = min(512, query_count)
    score_scale = HEAD_DIM ** (-0.5)

    def one_block(query_block):
        scores = jnp.dot(query_block, key_all.T, preferred_element_type=jnp.float32) * score_scale
        largest = jnp.max(scores, axis=1, keepdims=True)
        raised = jnp.exp(scores - largest)
        denominator = jnp.sum(raised, axis=1, keepdims=True)
        weights = raised.astype(jnp.bfloat16)
        mixed = jnp.dot(weights, value_all, preferred_element_type=jnp.float32)
        return (mixed / denominator).astype(jnp.bfloat16)

    blocks = lax.map(
        one_block, query_here.reshape(query_count // block_size, block_size, head_width)
    )
    return blocks.reshape(query_count, head_width)


ALL = ("side", "inner", "dp")


def local(queries, key_vectors, value_vectors, w_out, cotangent):
    head_count = HEADS
    head_width = HEAD_DIM
    side_count = lax.axis_size("side")
    dp_count = lax.axis_size("dp")
    row_count = queries.shape[1]
    width = queries.shape[2]

    dp_index = lax.axis_index("dp")
    w_full = lax.all_gather(w_out, ALL, axis=0, tiled=True)
    cot_side = lax.all_gather(cotangent[0], "inner", axis=0, tiled=True)

    def a2a(tensor):
        return lax.all_to_all(tensor, "inner", split_axis=0, concat_axis=0, tiled=True)

    def by_head(tensor):
        return tensor[0].reshape(row_count, head_count, head_width).transpose(1, 0, 2)

    side_index = lax.axis_index("side")
    kv_raw = jnp.concatenate([by_head(key_vectors), by_head(value_vectors)], axis=1)
    inner_index = lax.axis_index("inner")
    kv_crossed = []
    for step in range(1, side_count):
        for shift in range(head_count):
            perm = [
                (g * head_count + i, ((g + step) % side_count) * head_count + (i + shift) % head_count)
                for g in range(side_count)
                for i in range(head_count)
            ]
            outgoing = lax.dynamic_index_in_dim(
                kv_raw, (inner_index + shift) % head_count, axis=0, keepdims=False
            )
            kv_crossed.append(lax.ppermute(outgoing, ("side", "inner"), perm))
    stacked = jnp.concatenate([by_head(queries), kv_raw], axis=1)
    got = a2a(stacked)
    query_here = got[:, :row_count].reshape(head_count * row_count, head_width)
    key_parts = [got[:, row_count : 2 * row_count].reshape(-1, head_width)]
    value_parts = [got[:, 2 * row_count :].reshape(-1, head_width)]
    for crossed in kv_crossed:
        key_parts.append(crossed[:row_count])
        value_parts.append(crossed[row_count:])
    key_all = jnp.concatenate(key_parts, axis=0)
    value_all = jnp.concatenate(value_parts, axis=0)

    attended_here = attend(query_here, key_all, value_all)

    partial = lax.dot_general(
        attended_here, cot_side, (((0,), (0,)), ((), ())), preferred_element_type=jnp.float32
    )

    returned = a2a(attended_here.reshape(head_count, row_count, head_width))
    attended = returned.transpose(1, 0, 2).reshape(row_count, width)
    projected = jnp.dot(attended, w_full, preferred_element_type=jnp.float32).astype(
        jnp.bfloat16
    )

    chunk_count = side_count * dp_count
    chunk = head_width // chunk_count
    side_index = lax.axis_index("side")
    if dp_count == 2:
        pieces = partial.reshape(side_count, dp_count, chunk, width)
        kept = lax.dynamic_index_in_dim(pieces, dp_index, axis=1, keepdims=False)
        sent = lax.dynamic_index_in_dim(pieces, 1 - dp_index, axis=1, keepdims=False)
        kept = kept + lax.ppermute(sent, "dp", [(0, 1), (1, 0)])
        grad_w_out = None
        for step in range(side_count):
            perm = []
            for g in range(side_count):
                for h in range(head_count):
                    for p in range(dp_count):
                        owner_side = (g + step) % side_count
                        source = (g * head_count + h) * dp_count + p
                        target = (side_count * h + owner_side) * dp_count + p
                        perm.append((source, target))
            outgoing = lax.dynamic_index_in_dim(
                kept, (side_index + step) % side_count, axis=0, keepdims=False
            )
            arrived = lax.ppermute(outgoing, ALL, perm)
            grad_w_out = arrived if grad_w_out is None else grad_w_out + arrived
    else:
        pieces = partial.reshape(chunk_count, chunk, width)
        holder = side_index * dp_count + dp_index
        grad_w_out = None
        for step in range(chunk_count):
            perm = []
            for g in range(side_count):
                for h in range(head_count):
                    for p in range(dp_count):
                        c = (g * dp_count + p + step) % chunk_count
                        source = (g * head_count + h) * dp_count + p
                        target = (side_count * h + c // dp_count) * dp_count + c % dp_count
                        perm.append((source, target))
            outgoing = lax.dynamic_index_in_dim(
                pieces, (holder + step) % chunk_count, axis=0, keepdims=False
            )
            arrived = lax.ppermute(outgoing, ALL, perm)
            grad_w_out = arrived if grad_w_out is None else grad_w_out + arrived
    return (projected.reshape(1, row_count, width), grad_w_out)


def solution(mesh):
    seq_count = mesh.shape["seq"]
    dp_count = mesh.shape["dp"]
    fine = Mesh(
        mesh.devices.reshape(seq_count // HEADS, HEADS, dp_count), ("side", "inner", "dp")
    )
    seq = ("side", "inner")
    placed = (
        P("dp", seq, None),
        P("dp", seq, None),
        P("dp", seq, None),
        P(ALL, None),
        P("dp", seq, None),
    )
    return jax.shard_map(
        local,
        mesh=fine,
        in_specs=placed,
        out_specs=(P("dp", seq, None), P(ALL, None)),
        check_vma=False,
    )
```

```python
import jax
import jax.numpy as jnp
from jax import lax
from jax.sharding import Mesh
from jax.sharding import PartitionSpec as P

HEADS = 8
HEAD_DIM = 192


def attend(query_here, key_all, value_all):
    query_count = query_here.shape[0]
    head_width = query_here.shape[1]
    block_size = min(512, query_count)
    score_scale = HEAD_DIM ** (-0.5)

    def one_block(query_block):
        scores = jnp.dot(query_block, key_all.T, preferred_element_type=jnp.float32) * score_scale
        largest = jnp.max(scores, axis=1, keepdims=True)
        raised = jnp.exp(scores - largest)
        denominator = jnp.sum(raised, axis=1, keepdims=True)
        weights = raised.astype(jnp.bfloat16)
        mixed = jnp.dot(weights, value_all, preferred_element_type=jnp.float32)
        return (mixed / denominator).astype(jnp.bfloat16)

    blocks = lax.map(
        one_block, query_here.reshape(query_count // block_size, block_size, head_width)
    )
    return blocks.reshape(query_count, head_width)


ALL = ("side", "inner", "dp")


def local(queries, key_vectors, value_vectors, w_out, cotangent):
    head_count = HEADS
    head_width = HEAD_DIM
    side_count = lax.axis_size("side")
    dp_count = lax.axis_size("dp")
    row_count = queries.shape[1]
    width = queries.shape[2]

    dp_index = lax.axis_index("dp")
    w_full = lax.all_gather(w_out, ALL, axis=0, tiled=True)
    cot_side = lax.all_gather(cotangent[0], "inner", axis=0, tiled=True)

    def a2a(tensor):
        return lax.all_to_all(tensor, "inner", split_axis=0, concat_axis=0, tiled=True)

    half_heads = head_count // 2

    def head_of(j):
        return j // 2 + half_heads * (j % 2)

    def by_head(tensor):
        tensor = tensor[0].reshape(row_count, 2, half_heads, head_width).transpose(2, 1, 0, 3)
        return tensor.reshape(head_count, row_count, head_width)

    side_index = lax.axis_index("side")
    kv_raw = jnp.concatenate([by_head(key_vectors), by_head(value_vectors)], axis=2)
    inner_index = lax.axis_index("inner")
    kv_crossed = []
    for step in range(1, side_count):
        for shift in range(head_count):
            perm = [
                (g * head_count + i, ((g + step) % side_count) * head_count + (i + shift) % head_count)
                for g in range(side_count)
                for i in range(head_count)
            ]
            outgoing = lax.dynamic_index_in_dim(
                kv_raw, (inner_index + shift) % head_count, axis=0, keepdims=False
            )
            kv_crossed.append(lax.ppermute(outgoing, ("side", "inner"), perm))
    stacked = jnp.concatenate([by_head(queries), kv_raw], axis=2)
    got = a2a(stacked).reshape(head_count * row_count, 3 * head_width)
    query_here = got[:, :head_width]
    kv_all = jnp.concatenate([got[:, head_width:]] + kv_crossed, axis=0)
    key_all = kv_all[:, :head_width]
    value_all = kv_all[:, head_width:]

    attended_here = attend(query_here, key_all, value_all)

    partial = lax.dot_general(
        attended_here, cot_side, (((0,), (0,)), ((), ())), preferred_element_type=jnp.float32
    )

    returned = a2a(attended_here.reshape(head_count, row_count, head_width))
    attended = (
        returned.reshape(half_heads, 2, row_count, head_width)
        .transpose(2, 1, 0, 3)
        .reshape(row_count, width)
    )
    projected = jnp.dot(attended, w_full, preferred_element_type=jnp.float32).astype(
        jnp.bfloat16
    )

    chunk_count = side_count * dp_count
    chunk = head_width // chunk_count
    side_index = lax.axis_index("side")
    if dp_count == 2:
        pieces = partial.reshape(side_count, dp_count, chunk, width)
        kept = lax.dynamic_index_in_dim(pieces, dp_index, axis=1, keepdims=False)
        sent = lax.dynamic_index_in_dim(pieces, 1 - dp_index, axis=1, keepdims=False)
        kept = kept + lax.ppermute(sent, "dp", [(0, 1), (1, 0)])
        grad_w_out = None
        for step in range(side_count):
            perm = []
            for g in range(side_count):
                for h in range(head_count):
                    for p in range(dp_count):
                        owner_side = (g + step) % side_count
                        source = (g * head_count + h) * dp_count + p
                        target = (side_count * head_of(h) + owner_side) * dp_count + p
                        perm.append((source, target))
            outgoing = lax.dynamic_index_in_dim(
                kept, (side_index + step) % side_count, axis=0, keepdims=False
            )
            arrived = lax.ppermute(outgoing, ALL, perm)
            grad_w_out = arrived if grad_w_out is None else grad_w_out + arrived
    else:
        pieces = partial.reshape(chunk_count, chunk, width)
        holder = side_index * dp_count + dp_index
        grad_w_out = None
        for step in range(chunk_count):
            perm = []
            for g in range(side_count):
                for h in range(head_count):
                    for p in range(dp_count):
                        c = (g * dp_count + p + step) % chunk_count
                        source = (g * head_count + h) * dp_count + p
                        target = (side_count * head_of(h) + c // dp_count) * dp_count + c % dp_count
                        perm.append((source, target))
            outgoing = lax.dynamic_index_in_dim(
                pieces, (holder + step) % chunk_count, axis=0, keepdims=False
            )
            arrived = lax.ppermute(outgoing, ALL, perm)
            grad_w_out = arrived if grad_w_out is None else grad_w_out + arrived
    return (projected.reshape(1, row_count, width), grad_w_out)


def solution(mesh):
    seq_count = mesh.shape["seq"]
    dp_count = mesh.shape["dp"]
    fine = Mesh(
        mesh.devices.reshape(seq_count // HEADS, HEADS, dp_count), ("side", "inner", "dp")
    )
    seq = ("side", "inner")
    placed = (
        P("dp", seq, None),
        P("dp", seq, None),
        P("dp", seq, None),
        P(ALL, None),
        P("dp", seq, None),
    )
    return jax.shard_map(
        local,
        mesh=fine,
        in_specs=placed,
        out_specs=(P("dp", seq, None), P(ALL, None)),
        check_vma=False,
    )
```

```python
import jax
import jax.numpy as jnp
from jax import lax
from jax.sharding import Mesh
from jax.sharding import PartitionSpec as P

HEADS = 8
HEAD_DIM = 192


def attend(query_here, key_all, value_all):
    query_count = query_here.shape[0]
    head_width = query_here.shape[1]
    block_size = min(512, query_count)
    score_scale = HEAD_DIM ** (-0.5)

    def one_block(query_block):
        scores = jnp.dot(query_block, key_all.T, preferred_element_type=jnp.float32) * score_scale
        largest = jnp.max(scores, axis=1, keepdims=True)
        raised = jnp.exp(scores - largest)
        denominator = jnp.sum(raised, axis=1, keepdims=True)
        weights = raised.astype(jnp.bfloat16)
        mixed = jnp.dot(weights, value_all, preferred_element_type=jnp.float32)
        return (mixed / denominator).astype(jnp.bfloat16)

    blocks = lax.map(
        one_block, query_here.reshape(query_count // block_size, block_size, head_width)
    )
    return blocks.reshape(query_count, head_width)


ALL = ("side", "inner", "dp")


def local(queries, key_vectors, value_vectors, w_out, cotangent):
    head_count = HEADS
    head_width = HEAD_DIM
    side_count = lax.axis_size("side")
    dp_count = lax.axis_size("dp")
    row_count = queries.shape[1]
    width = queries.shape[2]

    dp_index = lax.axis_index("dp")
    w_full = lax.all_gather(w_out, ALL, axis=0, tiled=True)
    cot_side = lax.all_gather(cotangent[0], "inner", axis=0, tiled=True)

    def a2a(tensor):
        return lax.all_to_all(tensor, "inner", split_axis=0, concat_axis=0, tiled=True)

    half_heads = head_count // 2

    def head_of(j):
        return j // 2 + half_heads * (j % 2)

    def by_head(tensor):
        tensor = tensor[0].reshape(row_count, 2, half_heads, head_width).transpose(2, 1, 0, 3)
        return tensor.reshape(head_count, row_count, head_width)

    side_index = lax.axis_index("side")
    kv_raw = jnp.concatenate([by_head(key_vectors), by_head(value_vectors)], axis=2)
    inner_index = lax.axis_index("inner")
    kv_crossed = []
    for step in range(1, side_count):
        for shift in range(head_count):
            perm = [
                (g * head_count + i, ((g + step) % side_count) * head_count + (i + shift) % head_count)
                for g in range(side_count)
                for i in range(head_count)
            ]
            outgoing = lax.dynamic_index_in_dim(
                kv_raw, (inner_index + shift) % head_count, axis=0, keepdims=False
            )
            kv_crossed.append(lax.ppermute(outgoing, ("side", "inner"), perm))
    stacked = jnp.concatenate([by_head(queries), kv_raw], axis=2)
    got = a2a(stacked).reshape(head_count * row_count, 3 * head_width)
    query_here = got[:, :head_width]
    kv_all = jnp.concatenate([got[:, head_width:]] + kv_crossed, axis=0)
    key_all = kv_all[:, :head_width]
    value_all = kv_all[:, head_width:]

    attended_here = attend(query_here, key_all, value_all)

    partial = lax.dot_general(
        attended_here, cot_side, (((0,), (0,)), ((), ())), preferred_element_type=jnp.float32
    )

    partial, attended_back = lax.optimization_barrier((partial, attended_here))
    returned = a2a(attended_back.reshape(head_count, row_count, head_width))
    attended = (
        returned.reshape(half_heads, 2, row_count, head_width)
        .transpose(2, 1, 0, 3)
        .reshape(row_count, width)
    )
    projected = jnp.dot(attended, w_full, preferred_element_type=jnp.float32).astype(
        jnp.bfloat16
    )

    chunk_count = side_count * dp_count
    chunk = head_width // chunk_count
    side_index = lax.axis_index("side")
    if dp_count == 2:
        pieces = partial.reshape(side_count, dp_count, chunk, width)
        kept = lax.dynamic_index_in_dim(pieces, dp_index, axis=1, keepdims=False)
        sent = lax.dynamic_index_in_dim(pieces, 1 - dp_index, axis=1, keepdims=False)
        kept = kept + lax.ppermute(sent, "dp", [(0, 1), (1, 0)])
        grad_w_out = None
        for step in range(side_count):
            perm = []
            for g in range(side_count):
                for h in range(head_count):
                    for p in range(dp_count):
                        owner_side = (g + step) % side_count
                        source = (g * head_count + h) * dp_count + p
                        target = (side_count * head_of(h) + owner_side) * dp_count + p
                        perm.append((source, target))
            outgoing = lax.dynamic_index_in_dim(
                kept, (side_index + step) % side_count, axis=0, keepdims=False
            )
            arrived = lax.ppermute(outgoing, ALL, perm)
            grad_w_out = arrived if grad_w_out is None else grad_w_out + arrived
    else:
        pieces = partial.reshape(chunk_count, chunk, width)
        holder = side_index * dp_count + dp_index
        grad_w_out = None
        for step in range(chunk_count):
            perm = []
            for g in range(side_count):
                for h in range(head_count):
                    for p in range(dp_count):
                        c = (g * dp_count + p + step) % chunk_count
                        source = (g * head_count + h) * dp_count + p
                        target = (side_count * head_of(h) + c // dp_count) * dp_count + c % dp_count
                        perm.append((source, target))
            outgoing = lax.dynamic_index_in_dim(
                pieces, (holder + step) % chunk_count, axis=0, keepdims=False
            )
            arrived = lax.ppermute(outgoing, ALL, perm)
            grad_w_out = arrived if grad_w_out is None else grad_w_out + arrived
    return (projected.reshape(1, row_count, width), grad_w_out)


def solution(mesh):
    seq_count = mesh.shape["seq"]
    dp_count = mesh.shape["dp"]
    fine = Mesh(
        mesh.devices.reshape(seq_count // HEADS, HEADS, dp_count), ("side", "inner", "dp")
    )
    seq = ("side", "inner")
    placed = (
        P("dp", seq, None),
        P("dp", seq, None),
        P("dp", seq, None),
        P(ALL, None),
        P("dp", seq, None),
    )
    return jax.shard_map(
        local,
        mesh=fine,
        in_specs=placed,
        out_specs=(P("dp", seq, None), P(ALL, None)),
        check_vma=False,
    )
```

```python
import jax
import jax.numpy as jnp
from jax import lax
from jax.sharding import Mesh
from jax.sharding import PartitionSpec as P

HEADS = 8
HEAD_DIM = 192


def attend(query_here, key_all, value_all):
    query_count = query_here.shape[0]
    head_width = query_here.shape[1]
    block_size = min(512, query_count)
    score_scale = HEAD_DIM ** (-0.5)

    def one_block(query_block):
        scores = jnp.dot(query_block, key_all.T, preferred_element_type=jnp.float32) * score_scale
        largest = jnp.max(scores, axis=1, keepdims=True)
        raised = jnp.exp(scores - largest)
        denominator = jnp.sum(raised, axis=1, keepdims=True)
        weights = raised.astype(jnp.bfloat16)
        mixed = jnp.dot(weights, value_all, preferred_element_type=jnp.float32)
        return (mixed / denominator).astype(jnp.bfloat16)

    blocks = lax.map(
        one_block, query_here.reshape(query_count // block_size, block_size, head_width)
    )
    return blocks.reshape(query_count, head_width)


ALL = ("side", "inner", "dp")


def local(queries, key_vectors, value_vectors, w_out, cotangent):
    head_count = HEADS
    head_width = HEAD_DIM
    side_count = lax.axis_size("side")
    dp_count = lax.axis_size("dp")
    row_count = queries.shape[1]
    width = queries.shape[2]

    dp_index = lax.axis_index("dp")
    w_full = lax.all_gather(w_out, ALL, axis=0, tiled=True)
    cot_side = lax.all_gather(cotangent[0], "inner", axis=0, tiled=True)

    def a2a(tensor):
        return lax.all_to_all(tensor, "inner", split_axis=0, concat_axis=0, tiled=True)

    def by_head(tensor):
        return tensor[0].reshape(row_count, head_count, head_width).transpose(1, 0, 2)

    side_index = lax.axis_index("side")
    def by_lane(tensor):
        return tensor[0].reshape(row_count, head_count, head_width)

    kv_raw = jnp.concatenate([by_lane(key_vectors), by_lane(value_vectors)], axis=2)
    inner_index = lax.axis_index("inner")
    kv_crossed = []
    for step in range(1, side_count):
        for shift in range(head_count):
            perm = [
                (g * head_count + i, ((g + step) % side_count) * head_count + (i + shift) % head_count)
                for g in range(side_count)
                for i in range(head_count)
            ]
            outgoing = lax.dynamic_index_in_dim(
                kv_raw, (inner_index + shift) % head_count, axis=1, keepdims=False
            )
            kv_crossed.append(lax.ppermute(outgoing, ("side", "inner"), perm))
    stacked = jnp.concatenate([by_lane(queries), kv_raw], axis=2)
    got = lax.all_to_all(stacked, "inner", split_axis=1, concat_axis=0, tiled=True).reshape(
        head_count * row_count, 3 * head_width
    )
    query_here = got[:, :head_width]
    kv_all = jnp.concatenate([got[:, head_width:]] + kv_crossed, axis=0)
    key_all = kv_all[:, :head_width]
    value_all = kv_all[:, head_width:]

    attended_here = attend(query_here, key_all, value_all)

    partial = lax.dot_general(
        attended_here, cot_side, (((0,), (0,)), ((), ())), preferred_element_type=jnp.float32
    )

    returned = a2a(attended_here.reshape(head_count, row_count, head_width))
    attended = returned.transpose(1, 0, 2).reshape(row_count, width)
    projected = jnp.dot(attended, w_full, preferred_element_type=jnp.float32).astype(
        jnp.bfloat16
    )

    chunk_count = side_count * dp_count
    chunk = head_width // chunk_count
    side_index = lax.axis_index("side")
    if dp_count == 2:
        pieces = partial.reshape(side_count, dp_count, chunk, width)
        kept = lax.dynamic_index_in_dim(pieces, dp_index, axis=1, keepdims=False)
        sent = lax.dynamic_index_in_dim(pieces, 1 - dp_index, axis=1, keepdims=False)
        kept = kept + lax.ppermute(sent, "dp", [(0, 1), (1, 0)])
        grad_w_out = None
        for step in range(side_count):
            perm = []
            for g in range(side_count):
                for h in range(head_count):
                    for p in range(dp_count):
                        owner_side = (g + step) % side_count
                        source = (g * head_count + h) * dp_count + p
                        target = (side_count * h + owner_side) * dp_count + p
                        perm.append((source, target))
            outgoing = lax.dynamic_index_in_dim(
                kept, (side_index + step) % side_count, axis=0, keepdims=False
            )
            arrived = lax.ppermute(outgoing, ALL, perm)
            grad_w_out = arrived if grad_w_out is None else grad_w_out + arrived
    else:
        pieces = partial.reshape(chunk_count, chunk, width)
        holder = side_index * dp_count + dp_index
        grad_w_out = None
        for step in range(chunk_count):
            perm = []
            for g in range(side_count):
                for h in range(head_count):
                    for p in range(dp_count):
                        c = (g * dp_count + p + step) % chunk_count
                        source = (g * head_count + h) * dp_count + p
                        target = (side_count * h + c // dp_count) * dp_count + c % dp_count
                        perm.append((source, target))
            outgoing = lax.dynamic_index_in_dim(
                pieces, (holder + step) % chunk_count, axis=0, keepdims=False
            )
            arrived = lax.ppermute(outgoing, ALL, perm)
            grad_w_out = arrived if grad_w_out is None else grad_w_out + arrived
    return (projected.reshape(1, row_count, width), grad_w_out)


def solution(mesh):
    seq_count = mesh.shape["seq"]
    dp_count = mesh.shape["dp"]
    fine = Mesh(
        mesh.devices.reshape(seq_count // HEADS, HEADS, dp_count), ("side", "inner", "dp")
    )
    seq = ("side", "inner")
    placed = (
        P("dp", seq, None),
        P("dp", seq, None),
        P("dp", seq, None),
        P(ALL, None),
        P("dp", seq, None),
    )
    return jax.shard_map(
        local,
        mesh=fine,
        in_specs=placed,
        out_specs=(P("dp", seq, None), P(ALL, None)),
        check_vma=False,
    )
```

```python
import jax
import jax.numpy as jnp
from jax import lax
from jax.sharding import Mesh
from jax.sharding import PartitionSpec as P

HEADS = 8
HEAD_DIM = 192


def attend(query_here, key_all, value_all):
    query_count = query_here.shape[0]
    head_width = query_here.shape[1]
    block_size = min(512, query_count)
    score_scale = HEAD_DIM ** (-0.5)

    def one_block(query_block):
        scores = jnp.dot(query_block, key_all.T, preferred_element_type=jnp.float32) * score_scale
        largest = jnp.max(scores, axis=1, keepdims=True)
        raised = jnp.exp(scores - largest)
        denominator = jnp.sum(raised, axis=1, keepdims=True)
        weights = raised.astype(jnp.bfloat16)
        mixed = jnp.dot(weights, value_all, preferred_element_type=jnp.float32)
        return (mixed / denominator).astype(jnp.bfloat16)

    blocks = lax.map(
        one_block, query_here.reshape(query_count // block_size, block_size, head_width)
    )
    return blocks.reshape(query_count, head_width)


ALL = ("side", "inner", "dp")


def local(queries, key_vectors, value_vectors, w_out, cotangent):
    head_count = HEADS
    head_width = HEAD_DIM
    side_count = lax.axis_size("side")
    dp_count = lax.axis_size("dp")
    row_count = queries.shape[1]
    width = queries.shape[2]

    dp_index = lax.axis_index("dp")
    w_full = lax.all_gather(w_out, ALL, axis=0, tiled=True)
    cot_side = lax.all_gather(cotangent[0], "inner", axis=0, tiled=True)

    def a2a(tensor):
        return lax.all_to_all(tensor, "inner", split_axis=0, concat_axis=0, tiled=True)

    def by_head(tensor):
        return tensor[0].reshape(row_count, head_count, head_width).transpose(1, 0, 2)

    side_index = lax.axis_index("side")
    def by_lane(tensor):
        return tensor[0].reshape(row_count, head_count, head_width)

    kv_raw = jnp.concatenate([by_lane(key_vectors), by_lane(value_vectors)], axis=2)
    inner_index = lax.axis_index("inner")
    kv_crossed = []
    for step in range(1, side_count):
        for shift in range(head_count):
            perm = [
                (g * head_count + i, ((g + step) % side_count) * head_count + (i + shift) % head_count)
                for g in range(side_count)
                for i in range(head_count)
            ]
            outgoing = lax.dynamic_index_in_dim(
                kv_raw, (inner_index + shift) % head_count, axis=1, keepdims=False
            )
            kv_crossed.append(lax.ppermute(outgoing, ("side", "inner"), perm))
    stacked = jnp.concatenate([by_lane(queries), kv_raw], axis=2)
    got = lax.all_to_all(stacked, "inner", split_axis=1, concat_axis=0, tiled=True).reshape(
        head_count * row_count, 3 * head_width
    )
    early = min(3, len(kv_crossed))
    kv_early, got = lax.optimization_barrier((kv_crossed[:early], got))
    kv_crossed = list(kv_early) + kv_crossed[early:]
    query_here = got[:, :head_width]
    kv_all = jnp.concatenate([got[:, head_width:]] + kv_crossed, axis=0)
    key_all = kv_all[:, :head_width]
    value_all = kv_all[:, head_width:]

    attended_here = attend(query_here, key_all, value_all)

    partial = lax.dot_general(
        attended_here, cot_side, (((0,), (0,)), ((), ())), preferred_element_type=jnp.float32
    )

    returned = a2a(attended_here.reshape(head_count, row_count, head_width))
    attended = returned.transpose(1, 0, 2).reshape(row_count, width)
    projected = jnp.dot(attended, w_full, preferred_element_type=jnp.float32).astype(
        jnp.bfloat16
    )

    chunk_count = side_count * dp_count
    chunk = head_width // chunk_count
    side_index = lax.axis_index("side")
    if dp_count == 2:
        pieces = partial.reshape(side_count, dp_count, chunk, width)
        kept = lax.dynamic_index_in_dim(pieces, dp_index, axis=1, keepdims=False)
        sent = lax.dynamic_index_in_dim(pieces, 1 - dp_index, axis=1, keepdims=False)
        kept = kept + lax.ppermute(sent, "dp", [(0, 1), (1, 0)])
        grad_w_out = None
        for step in range(side_count):
            perm = []
            for g in range(side_count):
                for h in range(head_count):
                    for p in range(dp_count):
                        owner_side = (g + step) % side_count
                        source = (g * head_count + h) * dp_count + p
                        target = (side_count * h + owner_side) * dp_count + p
                        perm.append((source, target))
            outgoing = lax.dynamic_index_in_dim(
                kept, (side_index + step) % side_count, axis=0, keepdims=False
            )
            arrived = lax.ppermute(outgoing, ALL, perm)
            grad_w_out = arrived if grad_w_out is None else grad_w_out + arrived
    else:
        pieces = partial.reshape(chunk_count, chunk, width)
        holder = side_index * dp_count + dp_index
        grad_w_out = None
        for step in range(chunk_count):
            perm = []
            for g in range(side_count):
                for h in range(head_count):
                    for p in range(dp_count):
                        c = (g * dp_count + p + step) % chunk_count
                        source = (g * head_count + h) * dp_count + p
                        target = (side_count * h + c // dp_count) * dp_count + c % dp_count
                        perm.append((source, target))
            outgoing = lax.dynamic_index_in_dim(
                pieces, (holder + step) % chunk_count, axis=0, keepdims=False
            )
            arrived = lax.ppermute(outgoing, ALL, perm)
            grad_w_out = arrived if grad_w_out is None else grad_w_out + arrived
    return (projected.reshape(1, row_count, width), grad_w_out)


def solution(mesh):
    seq_count = mesh.shape["seq"]
    dp_count = mesh.shape["dp"]
    fine = Mesh(
        mesh.devices.reshape(seq_count // HEADS, HEADS, dp_count), ("side", "inner", "dp")
    )
    seq = ("side", "inner")
    placed = (
        P("dp", seq, None),
        P("dp", seq, None),
        P("dp", seq, None),
        P(ALL, None),
        P("dp", seq, None),
    )
    return jax.shard_map(
        local,
        mesh=fine,
        in_specs=placed,
        out_specs=(P("dp", seq, None), P(ALL, None)),
        check_vma=False,
    )
```

```python
import jax
import jax.numpy as jnp
from jax import lax
from jax.sharding import Mesh
from jax.sharding import PartitionSpec as P

HEADS = 8
HEAD_DIM = 192


def attend(query_here, key_all, value_all):
    query_count = query_here.shape[0]
    head_width = query_here.shape[1]
    block_size = min(512, query_count)
    score_scale = HEAD_DIM ** (-0.5)

    def one_block(query_block):
        scores = jnp.dot(query_block, key_all.T, preferred_element_type=jnp.float32) * score_scale
        largest = jnp.max(scores, axis=1, keepdims=True)
        raised = jnp.exp(scores - largest)
        denominator = jnp.sum(raised, axis=1, keepdims=True)
        weights = raised.astype(jnp.bfloat16)
        mixed = jnp.dot(weights, value_all, preferred_element_type=jnp.float32)
        return (mixed / denominator).astype(jnp.bfloat16)

    blocks = lax.map(
        one_block, query_here.reshape(query_count // block_size, block_size, head_width)
    )
    return blocks.reshape(query_count, head_width)


ALL = ("side", "inner", "dp")


def local(queries, key_vectors, value_vectors, w_out, cotangent):
    head_count = HEADS
    head_width = HEAD_DIM
    side_count = lax.axis_size("side")
    dp_count = lax.axis_size("dp")
    row_count = queries.shape[1]
    width = queries.shape[2]

    dp_index = lax.axis_index("dp")
    w_full = lax.all_gather(w_out, ALL, axis=0, tiled=True)
    cot_side = lax.all_gather(cotangent[0], "inner", axis=0, tiled=True)

    def a2a(tensor):
        return lax.all_to_all(tensor, "inner", split_axis=0, concat_axis=0, tiled=True)

    def by_head(tensor):
        return tensor[0].reshape(row_count, head_count, head_width).transpose(1, 0, 2)

    side_index = lax.axis_index("side")
    def by_lane(tensor):
        return tensor[0].reshape(row_count, head_count, head_width)

    kv_raw = jnp.concatenate([by_lane(key_vectors), by_lane(value_vectors)], axis=2)
    inner_index = lax.axis_index("inner")
    kv_crossed = []
    for step in range(1, side_count):
        for shift in range(head_count):
            perm = [
                (g * head_count + i, ((g + step) % side_count) * head_count + (i + shift) % head_count)
                for g in range(side_count)
                for i in range(head_count)
            ]
            outgoing = lax.dynamic_index_in_dim(
                kv_raw, (inner_index + shift) % head_count, axis=1, keepdims=False
            )
            kv_crossed.append(lax.ppermute(outgoing, ("side", "inner"), perm))
    stacked = jnp.concatenate([by_lane(queries), kv_raw], axis=2)
    got = lax.all_to_all(stacked, "inner", split_axis=1, concat_axis=0, tiled=True).reshape(
        head_count * row_count, 3 * head_width
    )
    early = len(kv_crossed)
    kv_early, got = lax.optimization_barrier((kv_crossed[:early], got))
    kv_crossed = list(kv_early) + kv_crossed[early:]
    query_here = got[:, :head_width]
    kv_all = jnp.concatenate([got[:, head_width:]] + kv_crossed, axis=0)
    key_all = kv_all[:, :head_width]
    value_all = kv_all[:, head_width:]

    attended_here = attend(query_here, key_all, value_all)

    partial = lax.dot_general(
        attended_here, cot_side, (((0,), (0,)), ((), ())), preferred_element_type=jnp.float32
    )

    returned = a2a(attended_here.reshape(head_count, row_count, head_width))
    attended = returned.transpose(1, 0, 2).reshape(row_count, width)
    projected = jnp.dot(attended, w_full, preferred_element_type=jnp.float32).astype(
        jnp.bfloat16
    )

    chunk_count = side_count * dp_count
    chunk = head_width // chunk_count
    side_index = lax.axis_index("side")
    if dp_count == 2:
        pieces = partial.reshape(side_count, dp_count, chunk, width)
        kept = lax.dynamic_index_in_dim(pieces, dp_index, axis=1, keepdims=False)
        sent = lax.dynamic_index_in_dim(pieces, 1 - dp_index, axis=1, keepdims=False)
        kept = kept + lax.ppermute(sent, "dp", [(0, 1), (1, 0)])
        grad_w_out = None
        for step in range(side_count):
            perm = []
            for g in range(side_count):
                for h in range(head_count):
                    for p in range(dp_count):
                        owner_side = (g + step) % side_count
                        source = (g * head_count + h) * dp_count + p
                        target = (side_count * h + owner_side) * dp_count + p
                        perm.append((source, target))
            outgoing = lax.dynamic_index_in_dim(
                kept, (side_index + step) % side_count, axis=0, keepdims=False
            )
            arrived = lax.ppermute(outgoing, ALL, perm)
            grad_w_out = arrived if grad_w_out is None else grad_w_out + arrived
    else:
        pieces = partial.reshape(chunk_count, chunk, width)
        holder = side_index * dp_count + dp_index
        grad_w_out = None
        for step in range(chunk_count):
            perm = []
            for g in range(side_count):
                for h in range(head_count):
                    for p in range(dp_count):
                        c = (g * dp_count + p + step) % chunk_count
                        source = (g * head_count + h) * dp_count + p
                        target = (side_count * h + c // dp_count) * dp_count + c % dp_count
                        perm.append((source, target))
            outgoing = lax.dynamic_index_in_dim(
                pieces, (holder + step) % chunk_count, axis=0, keepdims=False
            )
            arrived = lax.ppermute(outgoing, ALL, perm)
            grad_w_out = arrived if grad_w_out is None else grad_w_out + arrived
    return (projected.reshape(1, row_count, width), grad_w_out)


def solution(mesh):
    seq_count = mesh.shape["seq"]
    dp_count = mesh.shape["dp"]
    fine = Mesh(
        mesh.devices.reshape(seq_count // HEADS, HEADS, dp_count), ("side", "inner", "dp")
    )
    seq = ("side", "inner")
    placed = (
        P("dp", seq, None),
        P("dp", seq, None),
        P("dp", seq, None),
        P(ALL, None),
        P("dp", seq, None),
    )
    return jax.shard_map(
        local,
        mesh=fine,
        in_specs=placed,
        out_specs=(P("dp", seq, None), P(ALL, None)),
        check_vma=False,
    )
```

```python
import jax
import jax.numpy as jnp
from jax import lax
from jax.sharding import Mesh
from jax.sharding import PartitionSpec as P

HEADS = 8
HEAD_DIM = 192


def attend(query_here, key_all, value_all):
    query_count = query_here.shape[0]
    head_width = query_here.shape[1]
    block_size = min(512, query_count)
    score_scale = HEAD_DIM ** (-0.5)

    def one_block(query_block):
        scores = jnp.dot(query_block, key_all.T, preferred_element_type=jnp.float32) * score_scale
        largest = jnp.max(scores, axis=1, keepdims=True)
        raised = jnp.exp(scores - largest)
        denominator = jnp.sum(raised, axis=1, keepdims=True)
        weights = raised.astype(jnp.bfloat16)
        mixed = jnp.dot(weights, value_all, preferred_element_type=jnp.float32)
        return (mixed / denominator).astype(jnp.bfloat16)

    blocks = lax.map(
        one_block, query_here.reshape(query_count // block_size, block_size, head_width)
    )
    return blocks.reshape(query_count, head_width)


ALL = ("side", "inner", "dp")


def local(queries, key_vectors, value_vectors, w_out, cotangent):
    head_count = HEADS
    head_width = HEAD_DIM
    side_count = lax.axis_size("side")
    dp_count = lax.axis_size("dp")
    row_count = queries.shape[1]
    width = queries.shape[2]

    dp_index = lax.axis_index("dp")
    w_full = lax.all_gather(w_out, ALL, axis=0, tiled=True)
    cot_side = lax.all_gather(cotangent[0], "inner", axis=0, tiled=True)

    def a2a(tensor):
        return lax.all_to_all(tensor, "inner", split_axis=0, concat_axis=0, tiled=True)

    def by_head(tensor):
        return tensor[0].reshape(row_count, head_count, head_width).transpose(1, 0, 2)

    side_index = lax.axis_index("side")
    def by_lane(tensor):
        return tensor[0].reshape(row_count, head_count, head_width)

    kv_raw = jnp.concatenate([by_lane(key_vectors), by_lane(value_vectors)], axis=2)
    inner_index = lax.axis_index("inner")
    kv_crossed = []
    for step in range(1, side_count):
        for shift in range(head_count):
            perm = [
                (g * head_count + i, ((g + step) % side_count) * head_count + (i + shift) % head_count)
                for g in range(side_count)
                for i in range(head_count)
            ]
            outgoing = lax.dynamic_index_in_dim(
                kv_raw, (inner_index + shift) % head_count, axis=1, keepdims=False
            )
            kv_crossed.append(lax.ppermute(outgoing, ("side", "inner"), perm))
    stacked = jnp.concatenate([by_lane(queries), kv_raw], axis=2)
    got = lax.all_to_all(stacked, "inner", split_axis=1, concat_axis=0, tiled=True).reshape(
        head_count * row_count, 3 * head_width
    )
    early = min(3, len(kv_crossed))
    kv_early, got = lax.optimization_barrier((kv_crossed[:early], got))
    kv_crossed = list(kv_early) + kv_crossed[early:]
    query_here = got[:, :head_width]
    kv_all = jnp.concatenate([got[:, head_width:]] + kv_crossed, axis=0)
    key_all = kv_all[:, :head_width]
    value_all = kv_all[:, head_width:]

    attended_here = attend(query_here, key_all, value_all)

    partial = lax.dot_general(
        attended_here, cot_side, (((0,), (0,)), ((), ())), preferred_element_type=jnp.float32
    )

    returned = a2a(attended_here.reshape(head_count, row_count, head_width))

    chunk_count = side_count * dp_count
    chunk = head_width // chunk_count
    side_index = lax.axis_index("side")
    if dp_count == 2:
        pieces = partial.reshape(side_count, dp_count, chunk, width)
        kept = lax.dynamic_index_in_dim(pieces, dp_index, axis=1, keepdims=False)
        sent = lax.dynamic_index_in_dim(pieces, 1 - dp_index, axis=1, keepdims=False)
        kept = kept + lax.ppermute(sent, "dp", [(0, 1), (1, 0)])
        grad_w_out = None
        for step in range(side_count):
            perm = []
            for g in range(side_count):
                for h in range(head_count):
                    for p in range(dp_count):
                        owner_side = (g + step) % side_count
                        source = (g * head_count + h) * dp_count + p
                        target = (side_count * h + owner_side) * dp_count + p
                        perm.append((source, target))
            outgoing = lax.dynamic_index_in_dim(
                kept, (side_index + step) % side_count, axis=0, keepdims=False
            )
            _, returned = lax.optimization_barrier((outgoing, returned))
            arrived = lax.ppermute(outgoing, ALL, perm)
            grad_w_out = arrived if grad_w_out is None else grad_w_out + arrived
    else:
        pieces = partial.reshape(chunk_count, chunk, width)
        holder = side_index * dp_count + dp_index
        grad_w_out = None
        for step in range(chunk_count):
            perm = []
            for g in range(side_count):
                for h in range(head_count):
                    for p in range(dp_count):
                        c = (g * dp_count + p + step) % chunk_count
                        source = (g * head_count + h) * dp_count + p
                        target = (side_count * h + c // dp_count) * dp_count + c % dp_count
                        perm.append((source, target))
            outgoing = lax.dynamic_index_in_dim(
                pieces, (holder + step) % chunk_count, axis=0, keepdims=False
            )
            arrived = lax.ppermute(outgoing, ALL, perm)
            grad_w_out = arrived if grad_w_out is None else grad_w_out + arrived
    attended = returned.transpose(1, 0, 2).reshape(row_count, width)
    projected = jnp.dot(attended, w_full, preferred_element_type=jnp.float32).astype(
        jnp.bfloat16
    )
    return (projected.reshape(1, row_count, width), grad_w_out)


def solution(mesh):
    seq_count = mesh.shape["seq"]
    dp_count = mesh.shape["dp"]
    fine = Mesh(
        mesh.devices.reshape(seq_count // HEADS, HEADS, dp_count), ("side", "inner", "dp")
    )
    seq = ("side", "inner")
    placed = (
        P("dp", seq, None),
        P("dp", seq, None),
        P("dp", seq, None),
        P(ALL, None),
        P("dp", seq, None),
    )
    return jax.shard_map(
        local,
        mesh=fine,
        in_specs=placed,
        out_specs=(P("dp", seq, None), P(ALL, None)),
        check_vma=False,
    )
```
